32 devices in a mesh: groups: 2 (over y), dp: 16 (over z, x, core).
Axes of the slice: x: 2, y: 2, z: 4, core: 2. Of those that a mesh axis runs over, the one named last changes fastest.
Arguments:
- queries: bfloat16 [8192, 2048], P(('groups', 'dp')), parts along dimension 0, may hold values from -6 to 6
- grad_out: bfloat16 [8192, 2048], P(('groups', 'dp')), parts along dimension 0, may hold values from -60 to 60
- params: float32 [4096, 2048], P(('groups', 'dp')), parts along dimension 0, may hold values from -0.0625 to 0.0625
- first_moment: float32 [4096, 2048], P(('groups', 'dp')), parts along dimension 0, may hold values from -6 to 6
- second_moment: float32 [4096, 2048], P(('groups', 'dp')), parts along dimension 0, may hold values from 0.05 to 0.08
- key_params: float32 [4096, 2048], P(('groups', 'dp')), parts along dimension 0, may hold values from -0.0625 to 0.0625
- keys: bfloat16 [4096, 2048], P(('groups', 'dp')), parts along dimension 0, may hold values from -6 to 6
- perm: int32 [4096], P('groups'), parts along dimension 0, may hold values from 0 to 2047, as said below
- inv_perm: int32 [4096], P('groups'), parts along dimension 0, may hold values from 0 to 2047, as said below
- bn_gain: float32 [4096], P('groups'), parts along dimension 0, may hold values from 0.25 to 1.75
- bn_shift: float32 [4096], P('groups'), parts along dimension 0, may hold values from -3 to 3
- queue: bfloat16 [16, 2048, 2048], P('groups', 'dp'), parts along dimension 0, may hold values from -6 to 6
- slot: int32 [1], replicated, may hold values from 0 to 7
Outputs:
- new_params: float32 [4096, 2048], P(('groups', 'dp')), parts along dimension 0
- new_first: float32 [4096, 2048], P(('groups', 'dp')), parts along dimension 0
- new_second: float32 [4096, 2048], P(('groups', 'dp')), parts along dimension 0
- new_key: float32 [4096, 2048], P(('groups', 'dp')), parts along dimension 0
- new_queue: bfloat16 [16, 2048, 2048], P('groups', 'dp'), parts along dimension 0
The draws below stay inside these ranges and needn't reach their ends.
There are 2 independent parts, one for each index of `groups`. The reference program is written for one: setup_inputs(seed, part) draws one part's arguments, and reference() takes and returns one part's arrays. A program takes and returns all parts, laid end to end along the dimension named above; an argument that names none is the same for every part. Nothing has to cross between parts.
Inputs may be any that keep to these rules, and one draw needn't show every extreme that they name: perm is a permutation of 0 to 2047; each aligned block of 128 of its entries holds exactly 8 values from every aligned block of 128 values. inv_perm[perm[i]] = i for every i.
All inputs are finite; a program needn't handle non-finite values.
Results may differ from the reference program's by a relative error of at most 0.0025.
Values may be sent and summed in bfloat16 or wider, within the bound.
No kernel may reach another device: no remote copies, remote signals or barrier semaphores. Data moves between devices by JAX's collectives and lax.ppermute only.
A program may use at most 128 MiB of HBM per device.

```python
import jax
import jax.numpy as jnp
from jax import lax

D = 2048
KEY_DEV = 128
QBLK = 8
TOKENS = 4096
KEYS = 2048
N_DP = 16


def shuffle_tables(key):
    members = N_DP
    block_rows = KEY_DEV
    per_peer = KEY_DEV // N_DP
    root_key = jax.random.fold_in(key, 71)
    inner_keys = jax.random.split(jax.random.fold_in(root_key, 1), members)
    inner = jax.vmap(lambda single: jax.random.permutation(single, block_rows))(inner_keys).astype(jnp.int32)
    shifts = jax.random.randint(jax.random.fold_in(root_key, 2), (members,), 0, members)
    targets = jnp.arange(members, dtype=jnp.int32)[:, None]
    bucket = (targets - shifts[None, :]) % members
    columns = bucket[:, :, None] * per_peer + jnp.arange(per_peer, dtype=jnp.int32)[None, None, :]
    senders = jnp.arange(members, dtype=jnp.int32)[None, :, None]
    picked = inner[senders, columns]
    arrivals = (senders * block_rows + picked).reshape(members, block_rows)
    outer_keys = jax.random.split(jax.random.fold_in(root_key, 3), members)
    outer = jax.vmap(lambda single: jax.random.permutation(single, block_rows))(outer_keys).astype(jnp.int32)
    forward = jnp.take_along_axis(arrivals, outer, axis=1).reshape(-1).astype(jnp.int32)
    backward = jnp.zeros_like(forward).at[forward].set(jnp.arange(forward.shape[0], dtype=jnp.int32))
    return (forward, backward.astype(jnp.int32))


def draw_perm(key, part):
    return shuffle_tables(key)[0]


def draw_inv_perm(key, part):
    return shuffle_tables(key)[1]


def draw_grad_out(key, part):
    base_key = jax.random.fold_in(key, 211)
    values = jnp.clip(10.0 * jax.random.normal(base_key, (TOKENS, D), jnp.float32), -60.0, 60.0)
    return values.astype(jnp.bfloat16)


def draw_first_moment(key, part):
    sign_key = jax.random.fold_in(key, 307)
    size_key = jax.random.fold_in(key, 308)
    plus_minus = jnp.where(jax.random.bernoulli(sign_key, 0.5, (D, D)), 1.0, -1.0).astype(jnp.float32)
    magnitude = jax.random.uniform(size_key, (D, D), jnp.float32, 4.0, 6.0)
    return plus_minus * magnitude


def draw_second_moment(key, part):
    base_key = jax.random.fold_in(key, 409)
    exponent = jax.random.uniform(base_key, (D, D), jnp.float32, jnp.log(0.05), jnp.log(0.08))
    values = jnp.clip(jnp.exp(exponent), 0.05, 0.08)
    return values


def strengthened(drawn, key, source, target, blocks, factor):
    owner, partner = [(jnp.arange(drawn.shape[axis_at]) // (drawn.shape[axis_at] // blocks)).reshape([-1 if axis == axis_at else 1 for axis in range(drawn.ndim)]) for axis_at in (source, target)]
    chosen = jax.random.permutation(key, blocks)[partner]
    strong = (owner == chosen) | (owner == (partner + blocks // 2) % blocks)
    return jnp.where(strong, factor * drawn, drawn)


def block_levels(key, extent, shards, smallest, largest):
    def one(dim, shards_of):
        draws = jax.random.uniform(jax.random.fold_in(jax.random.fold_in(key, 6), dim), (shards_of,), jnp.float32, smallest / len(shards), largest / len(shards))
        return jnp.repeat(jnp.exp(draws), extent[dim] // shards_of).reshape((-1,) + (1,) * (len(extent) - dim - 1))

    loudness = one(*shards[0])
    for cut in shards[1:]:
        loudness = loudness * one(*cut)
    return loudness


def scatter_about(rng, dims, scale, bound, cuts=(), held_as=jnp.bfloat16):
    array = scale * jax.random.normal(rng, dims, jnp.float32)
    if cuts:
        array = array * block_levels(rng, dims, cuts, -0.22, 0.18)
    return jnp.clip(array, -bound, bound).astype(held_as)


def bell_draw_with(stream_key, dims, width, bound, shards, heavy, kind=jnp.bfloat16):
    result = width * jax.random.normal(stream_key, dims, jnp.float32)
    if shards:
        result = result * block_levels(stream_key, dims, shards, -0.22, 0.18)
    return jnp.clip(strengthened(result, jax.random.fold_in(stream_key, 3), *heavy), -bound, bound).astype(kind)


def setup_inputs(seed: int = 0, part: int = 0) -> dict:
    arg_keys = jax.random.split(jax.random.key(seed), 14)
    part_keys = jax.random.split(jax.random.fold_in(arg_keys[13], part), 14)
    return {
        "queries": bell_draw_with(part_keys[0], (TOKENS, D), 1.0, 6.0, ((0, 16),), (0, 1, 16, 2.0)),
        "grad_out": draw_grad_out(jax.random.fold_in(jax.random.fold_in(arg_keys[13], part), 71), part),
        "params": scatter_about(part_keys[2], (D, D), (4 * D) ** -0.5, 0.0625, ((0, 16),), jnp.float32),
        "first_moment": draw_first_moment(jax.random.fold_in(jax.random.fold_in(arg_keys[13], part), 71), part),
        "second_moment": draw_second_moment(jax.random.fold_in(jax.random.fold_in(arg_keys[13], part), 71), part),
        "key_params": scatter_about(part_keys[5], (D, D), (4 * D) ** -0.5, 0.0625, ((0, 16),), jnp.float32),
        "keys": scatter_about(part_keys[6], (KEYS, D), 1.0, 6.0, ((0, 16),)),
        "perm": draw_perm(jax.random.fold_in(jax.random.fold_in(arg_keys[13], part), 71), part),
        "inv_perm": draw_inv_perm(jax.random.fold_in(jax.random.fold_in(arg_keys[13], part), 71), part),
        "bn_gain": jnp.clip(1.0 + 0.15 * jax.random.normal(part_keys[9], (D,), jnp.float32), 0.25, 1.75),
        "bn_shift": scatter_about(part_keys[10], (D,), 0.5, 3.0, (), jnp.float32),
        "queue": scatter_about(part_keys[11], (QBLK, KEYS, D), 1.0, 6.0, ((1, 16),)),
        "slot": jax.random.randint(arg_keys[12], (1,), 0, QBLK).astype(jnp.int32),
    }


norm_epsilon = 1e-05
adam_epsilon = 1e-08
bias_first = 1.0 - 0.9 ** 10
bias_second = 1.0 - 0.999 ** 10

def reference(queries, grad_out, params, first_moment, second_moment, key_params, keys, perm, inv_perm, bn_gain, bn_shift, queue, slot):
    gradient = jnp.dot(queries.T, grad_out, preferred_element_type=jnp.float32) * (1.0 / jnp.sqrt(jnp.float32(TOKENS)))
    new_first = 0.9 * first_moment + 0.1 * gradient
    new_second = 0.999 * second_moment + 0.001 * gradient * gradient
    update = new_first / bias_first / (jnp.sqrt(new_second / bias_second) + adam_epsilon)
    new_params = params - 0.05 * (update + 0.1 * params)
    new_key = 0.99 * key_params + 0.01 * new_params
    key_weight = new_key.astype(jnp.bfloat16)
    shuffled = jnp.take(keys, perm, axis=0)
    codes = jnp.dot(shuffled, key_weight, preferred_element_type=jnp.float32).astype(jnp.bfloat16)
    values = codes.astype(jnp.float32).reshape(N_DP, KEY_DEV, D)
    center = lax.optimization_barrier(jnp.mean(values, axis=1, keepdims=True))
    spread = lax.optimization_barrier(jnp.mean(jnp.square(values - center), axis=1, keepdims=True))
    normed = jax.nn.relu((values - center) * lax.rsqrt(spread + norm_epsilon) * bn_gain + bn_shift)
    normed = normed.astype(jnp.bfloat16).reshape(KEYS, D)
    restored = jnp.take(normed, inv_perm, axis=0)
    new_queue = lax.dynamic_update_slice(queue, restored[None], (slot[0], jnp.int32(0), jnp.int32(0)))
    return (new_params, new_first, new_second, new_key, new_queue)
```

```python
import jax
import jax.numpy as jnp
from jax import lax
from jax.sharding import Mesh
from jax.sharding import PartitionSpec as P

norm_epsilon = 1e-05
adam_epsilon = 1e-08
bias_first = 1.0 - 0.9**10
bias_second = 1.0 - 0.999**10

DP = ("zo", "xl", "c")


def route(mapping, position, block_rows, per_peer):
    members = mapping.shape[0] // block_rows
    layout = mapping.reshape(members, block_rows)
    owned = (layout // block_rows == position).astype(jnp.int32)
    ordinal = jnp.cumsum(owned, axis=1) - 1
    destination = jnp.arange(members, dtype=jnp.int32)[:, None] * per_peer + ordinal
    destination = jnp.where(owned == 1, destination, members * per_peer)
    offsets = jnp.where(owned == 1, layout - position * block_rows, 0)
    send_index = (
        jnp.zeros((members * per_peer + 1,), jnp.int32)
        .at[destination.reshape(-1)]
        .set(offsets.reshape(-1))[: members * per_peer]
    )
    own_block = lax.dynamic_slice_in_dim(mapping, position * block_rows, block_rows)
    anchor = own_block // block_rows
    indicator = (anchor[:, None] == jnp.arange(members, dtype=jnp.int32)[None, :]).astype(jnp.int32)
    arrival = jnp.sum((jnp.cumsum(indicator, axis=0) - 1) * indicator, axis=1)
    return (send_index, anchor * per_peer + arrival)


def pair_gradient(queries, grad_out):
    tokens, width = queries.shape
    zo = lax.axis_size("zo")
    x = lax.axis_index("xl")
    blocks = queries.reshape(tokens, zo, 2, 2, width // (4 * zo))
    mine = lax.dynamic_index_in_dim(blocks, x, axis=2, keepdims=False)
    theirs = lax.dynamic_index_in_dim(blocks, 1 - x, axis=2, keepdims=False)
    mine = mine.reshape(tokens, width // 2)
    theirs = theirs.reshape(tokens, width // 2)
    swap = [(0, 1), (1, 0)]
    got_queries, got_grad = lax.ppermute((theirs, grad_out), "xl", swap)
    both_queries = jnp.concatenate([mine, got_queries], axis=0)
    both_grad = jnp.concatenate([grad_out, got_grad], axis=0)
    partial = lax.dot_general(
        both_queries, both_grad, (((0,), (0,)), ((), ())), preferred_element_type=jnp.float32
    )
    return lax.psum_scatter(partial, ("zo", "c"), scatter_dimension=0, tiled=True)


def adamw(gradient, params, first_moment, second_moment, key_params):
    new_first = 0.9 * first_moment + 0.1 * gradient
    new_second = 0.999 * second_moment + 0.001 * gradient * gradient
    update = new_first / bias_first / (jnp.sqrt(new_second / bias_second) + adam_epsilon)
    new_params = params - 0.05 * (update + 0.1 * params)
    new_key = 0.99 * key_params + 0.01 * new_params
    return (new_params, new_first, new_second, new_key)


def batch_norm(codes, bn_gain, bn_shift):
    values = codes.astype(jnp.float32)
    center = jnp.mean(values, axis=0)
    spread = jnp.mean(jnp.square(values - center), axis=0)
    return jax.nn.relu(
        (values - center) * lax.rsqrt(spread + norm_epsilon) * bn_gain + bn_shift
    ).astype(jnp.bfloat16)


def per_device(
    queries,
    grad_out,
    params,
    first_moment,
    second_moment,
    key_params,
    keys,
    perm,
    inv_perm,
    bn_gain,
    bn_shift,
    queue,
    slot,
):
    position = lax.axis_index(DP)
    members = lax.axis_size(DP)
    block_rows = keys.shape[0]
    per_peer = block_rows // members
    scaling = 1.0 / jnp.sqrt(jnp.float32(queries.shape[0] * members))
    send_forward, receive_forward = route(perm, position, block_rows, per_peer)
    send_back, receive_back = route(inv_perm, position, block_rows, per_peer)
    moved = lax.all_to_all(
        jnp.take(keys, send_forward, axis=0), DP, split_axis=0, concat_axis=0, tiled=True
    )
    encoded_rows = jnp.take(moved, receive_forward, axis=0)
    gradient = pair_gradient(queries, grad_out) * scaling
    new_params, new_first, new_second, new_key = adamw(
        gradient, params, first_moment, second_moment, key_params
    )
    codes = jnp.dot(
        encoded_rows,
        lax.all_gather(new_key.astype(jnp.bfloat16), DP, axis=0, tiled=True),
        preferred_element_type=jnp.float32,
    )
    codes = codes.astype(jnp.bfloat16)
    normed = batch_norm(codes, bn_gain, bn_shift)
    returned = lax.all_to_all(
        jnp.take(normed, send_back, axis=0), DP, split_axis=0, concat_axis=0, tiled=True
    )
    restored = jnp.take(returned, receive_back, axis=0)
    new_queue = lax.dynamic_update_slice(
        queue, restored[None], (slot[0], jnp.int32(0), jnp.int32(0))
    )
    return (new_params, new_first, new_second, new_key, new_queue)


def solution(mesh):
    groups, dp = mesh.devices.shape
    grid = Mesh(mesh.devices.reshape(groups, dp // 4, 2, 2), ("groups",) + DP)
    rows = P(("groups",) + DP, None)
    in_specs = (
        rows,
        rows,
        rows,
        rows,
        rows,
        rows,
        rows,
        P("groups"),
        P("groups"),
        P("groups"),
        P("groups"),
        P("groups", DP, None),
        P(),
    )
    out_specs = (rows, rows, rows, rows, P("groups", DP, None))
    return jax.shard_map(
        per_device, mesh=grid, in_specs=in_specs, out_specs=out_specs, check_vma=False
    )
```

```python
import jax
import jax.numpy as jnp
from jax import lax
from jax.sharding import Mesh
from jax.sharding import PartitionSpec as P

norm_epsilon = 1e-05
adam_epsilon = 1e-08
bias_first = 1.0 - 0.9**10
bias_second = 1.0 - 0.999**10

DP = ("zo", "xl", "c")


def route(mapping, position, block_rows, per_peer):
    members = mapping.shape[0] // block_rows
    layout = mapping.reshape(members, block_rows)
    owned = layout // block_rows == position
    ordinal = jnp.cumsum(owned.astype(jnp.int32), axis=1) - 1
    offsets = layout - position * block_rows
    slots = jnp.arange(per_peer, dtype=jnp.int32)[None, :, None]
    hit = owned[:, None, :] & (ordinal[:, None, :] == slots)
    send_index = jnp.sum(jnp.where(hit, offsets[:, None, :], 0), axis=2).reshape(-1)
    own_block = lax.dynamic_slice_in_dim(mapping, position * block_rows, block_rows)
    anchor = own_block // block_rows
    indicator = (anchor[:, None] == jnp.arange(members, dtype=jnp.int32)[None, :]).astype(jnp.int32)
    arrival = jnp.sum((jnp.cumsum(indicator, axis=0) - 1) * indicator, axis=1)
    return (send_index, anchor * per_peer + arrival)


def pair_gradient(queries, grad_out, early):
    tokens, width = queries.shape
    zo = lax.axis_size("zo")
    x = lax.axis_index("xl")
    blocks = queries.reshape(tokens, zo, 2, 2, width // (4 * zo)).transpose(0, 2, 3, 1, 4)
    mine = lax.dynamic_index_in_dim(blocks, x, axis=1, keepdims=False)
    theirs = lax.dynamic_index_in_dim(blocks, 1 - x, axis=1, keepdims=False)
    mine = mine.reshape(tokens, width // 2)
    theirs = theirs.reshape(tokens, width // 2)
    swap = [(0, 1), (1, 0)]
    got_queries, got_grad = lax.ppermute((theirs, grad_out), "xl", swap)
    (got_queries, got_grad), early = lax.optimization_barrier(((got_queries, got_grad), early))
    both_queries = jnp.concatenate([mine, got_queries], axis=0)
    both_grad = jnp.concatenate([grad_out, got_grad], axis=0)
    partial = lax.dot_general(
        both_queries, both_grad, (((0,), (0,)), ((), ())), preferred_element_type=jnp.float32
    )
    partial = lax.psum_scatter(partial, "c", scatter_dimension=0, tiled=True)
    return lax.psum_scatter(partial, "zo", scatter_dimension=0, tiled=True), early


def adamw(gradient, params, first_moment, second_moment, key_params):
    new_first = 0.9 * first_moment + 0.1 * gradient
    new_second = 0.999 * second_moment + 0.001 * gradient * gradient
    update = new_first / bias_first / (jnp.sqrt(new_second / bias_second) + adam_epsilon)
    new_params = params - 0.05 * (update + 0.1 * params)
    new_key = 0.99 * key_params + 0.01 * new_params
    return (new_params, new_first, new_second, new_key)


def batch_norm(codes, bn_gain, bn_shift):
    values = codes.astype(jnp.float32)
    center = jnp.mean(values, axis=0)
    spread = jnp.mean(jnp.square(values - center), axis=0)
    return jax.nn.relu(
        (values - center) * lax.rsqrt(spread + norm_epsilon) * bn_gain + bn_shift
    ).astype(jnp.bfloat16)


def per_device(
    queries,
    grad_out,
    params,
    first_moment,
    second_moment,
    key_params,
    keys,
    perm,
    inv_perm,
    bn_gain,
    bn_shift,
    queue,
    slot,
):
    position = lax.axis_index(DP)
    members = lax.axis_size(DP)
    block_rows = keys.shape[0]
    per_peer = block_rows // members
    scaling = 1.0 / jnp.sqrt(jnp.float32(queries.shape[0] * members))
    send_forward, receive_forward = route(perm, position, block_rows, per_peer)
    send_back, receive_back = route(inv_perm, position, block_rows, per_peer)
    moved = lax.all_to_all(
        jnp.take(keys, send_forward, axis=0), DP, split_axis=0, concat_axis=0, tiled=True
    )
    encoded_rows = jnp.take(moved, receive_forward, axis=0)
    gradient, (encoded_rows, send_back, receive_back) = pair_gradient(
        queries, grad_out, (encoded_rows, send_back, receive_back)
    )
    new_params, new_first, new_second, new_key = adamw(
        gradient * scaling, params, first_moment, second_moment, key_params
    )
    zo = lax.axis_size("zo")
    weight = lax.all_gather(new_key.astype(jnp.bfloat16), ("zo", "xl"), axis=0, tiled=True)
    weight = lax.all_gather(weight, "c", axis=0, tiled=True)
    columns = encoded_rows.reshape(block_rows, zo, 2, 2, -1).transpose(0, 3, 1, 2, 4)
    codes = jnp.dot(
        columns.reshape(block_rows, -1), weight, preferred_element_type=jnp.float32
    )
    codes = codes.astype(jnp.bfloat16)
    normed = batch_norm(codes, bn_gain, bn_shift)
    returned = lax.all_to_all(
        jnp.take(normed, send_back, axis=0), DP, split_axis=0, concat_axis=0, tiled=True
    )
    restored = jnp.take(returned, receive_back, axis=0)
    new_queue = lax.dynamic_update_slice(
        queue, restored[None], (slot[0], jnp.int32(0), jnp.int32(0))
    )
    return (new_params, new_first, new_second, new_key, new_queue)


def solution(mesh):
    groups, dp = mesh.devices.shape
    grid = Mesh(mesh.devices.reshape(groups, dp // 4, 2, 2), ("groups",) + DP)
    rows = P(("groups",) + DP, None)
    in_specs = (
        rows,
        rows,
        rows,
        rows,
        rows,
        rows,
        rows,
        P("groups"),
        P("groups"),
        P("groups"),
        P("groups"),
        P("groups", DP, None),
        P(),
    )
    out_specs = (rows, rows, rows, rows, P("groups", DP, None))
    return jax.shard_map(
        per_device, mesh=grid, in_specs=in_specs, out_specs=out_specs, check_vma=False
    )
```

```python
import jax
import jax.numpy as jnp
from jax import lax
from jax.sharding import Mesh
from jax.sharding import PartitionSpec as P

norm_epsilon = 1e-05
adam_epsilon = 1e-08
bias_first = 1.0 - 0.9**10
bias_second = 1.0 - 0.999**10

DP = ("zo", "xl", "c")


def route(mapping, position, block_rows, per_peer):
    members = mapping.shape[0] // block_rows
    layout = mapping.reshape(members, block_rows)
    owned = layout // block_rows == position
    ordinal = jnp.cumsum(owned.astype(jnp.int32), axis=1) - 1
    offsets = layout - position * block_rows
    slots = jnp.arange(per_peer, dtype=jnp.int32)[None, :, None]
    hit = owned[:, None, :] & (ordinal[:, None, :] == slots)
    send_index = jnp.sum(jnp.where(hit, offsets[:, None, :], 0), axis=2).reshape(-1)
    own_block = lax.dynamic_slice_in_dim(mapping, position * block_rows, block_rows)
    anchor = own_block // block_rows
    indicator = (anchor[:, None] == jnp.arange(members, dtype=jnp.int32)[None, :]).astype(jnp.int32)
    arrival = jnp.sum((jnp.cumsum(indicator, axis=0) - 1) * indicator, axis=1)
    return (send_index, anchor * per_peer + arrival)


def pair_gradient(queries, grad_out):
    tokens, width = queries.shape
    zo = lax.axis_size("zo")
    x = lax.axis_index("xl")
    blocks = queries.reshape(tokens, zo, 2, 2, width // (4 * zo))
    mine = lax.dynamic_index_in_dim(blocks, x, axis=2, keepdims=False)
    theirs = lax.dynamic_index_in_dim(blocks, 1 - x, axis=2, keepdims=False)
    mine = mine.reshape(tokens, width // 2)
    theirs = theirs.reshape(tokens, width // 2)
    swap = [(0, 1), (1, 0)]
    got_queries, got_grad = lax.ppermute((theirs, grad_out), "xl", swap)
    both_queries = jnp.concatenate([mine, got_queries], axis=0)
    both_grad = jnp.concatenate([grad_out, got_grad], axis=0)
    partial = lax.dot_general(
        both_queries, both_grad, (((0,), (0,)), ((), ())), preferred_element_type=jnp.float32
    )
    return lax.psum_scatter(partial, ("zo", "c"), scatter_dimension=0, tiled=True)


def ring_codes(weight, rows):
    zo_size = lax.axis_size("zo")
    length = 2 * zo_size
    block = weight.shape[0]

    def where(q):
        return (q if q < zo_size else length - 1 - q, 0 if q < zo_size else 1)

    def index(zo, xl, c):
        return (zo * 2 + xl) * 2 + c

    def pairs(step):
        return [
            (index(*where(q), c), index(*where((q + step) % length), c))
            for q in range(length)
            for c in (0, 1)
        ]

    forward, backward = pairs(1), pairs(length - 1)
    partner = [
        (index(zo, xl, c), index(zo, xl, 1 - c))
        for zo in range(zo_size)
        for xl in (0, 1)
        for c in (0, 1)
    ]
    zo = lax.axis_index("zo")
    xl = lax.axis_index("xl")
    c = lax.axis_index("c")
    here = jnp.where(xl == 0, zo, length - 1 - zo)

    def columns(offset, cls):
        q = (here + offset) % length
        source = jnp.where(q < zo_size, q, length - 1 - q)
        source = (source * 2 + (q >= zo_size).astype(jnp.int32)) * 2 + cls
        return lax.dynamic_slice_in_dim(rows, source * block, block, axis=1)

    def add(total, offset, cls, shard):
        part = jnp.dot(columns(offset, cls), shard, preferred_element_type=jnp.float32)
        return part if total is None else total + part

    total = add(None, 0, c, weight)
    ahead, behind = weight, weight
    handed = [(0, weight)]
    for step in range(1, length // 2 + 1):
        sent = lax.ppermute(tuple(s for _, s in handed), DP, partner)
        for (offset, _), shard in zip(handed, sent):
            total = add(total, offset, 1 - c, shard)
        handed = []
        ahead = lax.ppermute(ahead, DP, forward)
        total = add(total, -step, c, ahead)
        handed.append((-step, ahead))
        if step < length // 2:
            behind = lax.ppermute(behind, DP, backward)
            total = add(total, step, c, behind)
            handed.append((step, behind))
    sent = lax.ppermute(tuple(s for _, s in handed), DP, partner)
    for (offset, _), shard in zip(handed, sent):
        total = add(total, offset, 1 - c, shard)
    return total


def adamw(gradient, params, first_moment, second_moment, key_params):
    new_first = 0.9 * first_moment + 0.1 * gradient
    new_second = 0.999 * second_moment + 0.001 * gradient * gradient
    update = new_first / bias_first / (jnp.sqrt(new_second / bias_second) + adam_epsilon)
    new_params = params - 0.05 * (update + 0.1 * params)
    new_key = 0.99 * key_params + 0.01 * new_params
    return (new_params, new_first, new_second, new_key)


def batch_norm(codes, bn_gain, bn_shift):
    values = codes.astype(jnp.float32)
    center = jnp.mean(values, axis=0)
    spread = jnp.mean(jnp.square(values - center), axis=0)
    return jax.nn.relu(
        (values - center) * lax.rsqrt(spread + norm_epsilon) * bn_gain + bn_shift
    ).astype(jnp.bfloat16)


def per_device(
    queries,
    grad_out,
    params,
    first_moment,
    second_moment,
    key_params,
    keys,
    perm,
    inv_perm,
    bn_gain,
    bn_shift,
    queue,
    slot,
):
    position = lax.axis_index(DP)
    members = lax.axis_size(DP)
    block_rows = keys.shape[0]
    per_peer = block_rows // members
    scaling = 1.0 / jnp.sqrt(jnp.float32(queries.shape[0] * members))
    send_forward, receive_forward = route(perm, position, block_rows, per_peer)
    send_back, receive_back = route(inv_perm, position, block_rows, per_peer)
    moved = lax.all_to_all(
        jnp.take(keys, send_forward, axis=0), DP, split_axis=0, concat_axis=0, tiled=True
    )
    encoded_rows = jnp.take(moved, receive_forward, axis=0)
    gradient = pair_gradient(queries, grad_out) * scaling
    gradient, (encoded_rows, send_back, receive_back) = lax.optimization_barrier(
        (gradient, (encoded_rows, send_back, receive_back))
    )
    new_params, new_first, new_second, new_key = adamw(
        gradient, params, first_moment, second_moment, key_params
    )
    codes = ring_codes(new_key.astype(jnp.bfloat16), encoded_rows)
    codes = codes.astype(jnp.bfloat16)
    normed = batch_norm(codes, bn_gain, bn_shift)
    returned = lax.all_to_all(
        jnp.take(normed, send_back, axis=0), DP, split_axis=0, concat_axis=0, tiled=True
    )
    restored = jnp.take(returned, receive_back, axis=0)
    new_queue = lax.dynamic_update_slice(
        queue, restored[None], (slot[0], jnp.int32(0), jnp.int32(0))
    )
    return (new_params, new_first, new_second, new_key, new_queue)


def solution(mesh):
    groups, dp = mesh.devices.shape
    grid = Mesh(mesh.devices.reshape(groups, dp // 4, 2, 2), ("groups",) + DP)
    rows = P(("groups",) + DP, None)
    in_specs = (
        rows,
        rows,
        rows,
        rows,
        rows,
        rows,
        rows,
        P("groups"),
        P("groups"),
        P("groups"),
        P("groups"),
        P("groups", DP, None),
        P(),
    )
    out_specs = (rows, rows, rows, rows, P("groups", DP, None))
    return jax.shard_map(
        per_device, mesh=grid, in_specs=in_specs, out_specs=out_specs, check_vma=False
    )
```

```python
import jax
import jax.numpy as jnp
from jax import lax
from jax.sharding import Mesh
from jax.sharding import PartitionSpec as P

norm_epsilon = 1e-05
adam_epsilon = 1e-08
bias_first = 1.0 - 0.9**10
bias_second = 1.0 - 0.999**10

DP = ("zo", "xl", "c")


def route(mapping, position, block_rows, per_peer):
    members = mapping.shape[0] // block_rows
    layout = mapping.reshape(members, block_rows)
    owned = layout // block_rows == position
    ordinal = jnp.cumsum(owned.astype(jnp.int32), axis=1) - 1
    offsets = layout - position * block_rows
    slots = jnp.arange(per_peer, dtype=jnp.int32)[None, :, None]
    hit = owned[:, None, :] & (ordinal[:, None, :] == slots)
    send_index = jnp.sum(jnp.where(hit, offsets[:, None, :], 0), axis=2).reshape(-1)
    own_block = lax.dynamic_slice_in_dim(mapping, position * block_rows, block_rows)
    anchor = own_block // block_rows
    indicator = (anchor[:, None] == jnp.arange(members, dtype=jnp.int32)[None, :]).astype(jnp.int32)
    arrival = jnp.sum((jnp.cumsum(indicator, axis=0) - 1) * indicator, axis=1)
    return (send_index, anchor * per_peer + arrival)


def pair_gradient(queries, grad_out):
    tokens, width = queries.shape
    zo = lax.axis_size("zo")
    x = lax.axis_index("xl")
    blocks = queries.reshape(tokens, zo, 2, 2, width // (4 * zo))
    mine = lax.dynamic_index_in_dim(blocks, x, axis=2, keepdims=False)
    theirs = lax.dynamic_index_in_dim(blocks, 1 - x, axis=2, keepdims=False)
    mine = mine.reshape(tokens, width // 2)
    theirs = theirs.reshape(tokens, width // 2)
    swap = [(0, 1), (1, 0)]
    half = grad_out.shape[1] // 2
    got_queries, got_first = lax.ppermute((theirs, grad_out[:, :half]), "xl", swap)
    got_second = lax.ppermute(grad_out[:, half:], "xl", swap)
    both_queries = jnp.concatenate([mine, got_queries], axis=0)
    parts = []
    for own, got in ((grad_out[:, :half], got_first), (grad_out[:, half:], got_second)):
        partial = lax.dot_general(
            both_queries,
            jnp.concatenate([own, got], axis=0),
            (((0,), (0,)), ((), ())),
            preferred_element_type=jnp.float32,
        )
        parts.append(lax.psum_scatter(partial, ("zo", "c"), scatter_dimension=0, tiled=True))
    return jnp.concatenate(parts, axis=1)


def ring_codes(weight, rows):
    zo_size = lax.axis_size("zo")
    length = 2 * zo_size
    block = weight.shape[0]

    def where(q):
        return (q if q < zo_size else length - 1 - q, 0 if q < zo_size else 1)

    def index(zo, xl, c):
        return (zo * 2 + xl) * 2 + c

    def pairs(step):
        return [
            (index(*where(q), c), index(*where((q + step) % length), c))
            for q in range(length)
            for c in (0, 1)
        ]

    forward, backward = pairs(1), pairs(length - 1)
    partner = [
        (index(zo, xl, c), index(zo, xl, 1 - c))
        for zo in range(zo_size)
        for xl in (0, 1)
        for c in (0, 1)
    ]
    zo = lax.axis_index("zo")
    xl = lax.axis_index("xl")
    c = lax.axis_index("c")
    here = jnp.where(xl == 0, zo, length - 1 - zo)

    def columns(offset, cls):
        q = (here + offset) % length
        source = jnp.where(q < zo_size, q, length - 1 - q)
        source = (source * 2 + (q >= zo_size).astype(jnp.int32)) * 2 + cls
        return lax.dynamic_slice_in_dim(rows, source * block, block, axis=1)

    def add(total, offset, cls, shard):
        part = jnp.dot(columns(offset, cls), shard, preferred_element_type=jnp.float32)
        return part if total is None else total + part

    total = add(None, 0, c, weight)
    ahead, behind = weight, weight
    handed = [(0, weight)]
    for step in range(1, length // 2 + 1):
        sent = lax.ppermute(tuple(s for _, s in handed), DP, partner)
        for (offset, _), shard in zip(handed, sent):
            total = add(total, offset, 1 - c, shard)
        handed = []
        ahead = lax.ppermute(ahead, DP, forward)
        total = add(total, -step, c, ahead)
        handed.append((-step, ahead))
        if step < length // 2:
            behind = lax.ppermute(behind, DP, backward)
            total = add(total, step, c, behind)
            handed.append((step, behind))
    sent = lax.ppermute(tuple(s for _, s in handed), DP, partner)
    for (offset, _), shard in zip(handed, sent):
        total = add(total, offset, 1 - c, shard)
    return total


def adamw(gradient, params, first_moment, second_moment, key_params):
    new_first = 0.9 * first_moment + 0.1 * gradient
    new_second = 0.999 * second_moment + 0.001 * gradient * gradient
    update = new_first / bias_first / (jnp.sqrt(new_second / bias_second) + adam_epsilon)
    new_params = params - 0.05 * (update + 0.1 * params)
    new_key = 0.99 * key_params + 0.01 * new_params
    return (new_params, new_first, new_second, new_key)


def batch_norm(codes, bn_gain, bn_shift):
    values = codes.astype(jnp.float32)
    center = jnp.mean(values, axis=0)
    spread = jnp.mean(jnp.square(values - center), axis=0)
    return jax.nn.relu(
        (values - center) * lax.rsqrt(spread + norm_epsilon) * bn_gain + bn_shift
    ).astype(jnp.bfloat16)


def per_device(
    queries,
    grad_out,
    params,
    first_moment,
    second_moment,
    key_params,
    keys,
    perm,
    inv_perm,
    bn_gain,
    bn_shift,
    queue,
    slot,
):
    position = lax.axis_index(DP)
    members = lax.axis_size(DP)
    block_rows = keys.shape[0]
    per_peer = block_rows // members
    scaling = 1.0 / jnp.sqrt(jnp.float32(queries.shape[0] * members))
    send_forward, receive_forward = route(perm, position, block_rows, per_peer)
    send_back, receive_back = route(inv_perm, position, block_rows, per_peer)
    moved = lax.all_to_all(
        jnp.take(keys, send_forward, axis=0), DP, split_axis=0, concat_axis=0, tiled=True
    )
    encoded_rows = jnp.take(moved, receive_forward, axis=0)
    gradient = pair_gradient(queries, grad_out) * scaling
    gradient, (encoded_rows, send_back, receive_back) = lax.optimization_barrier(
        (gradient, (encoded_rows, send_back, receive_back))
    )
    new_params, new_first, new_second, new_key = adamw(
        gradient, params, first_moment, second_moment, key_params
    )
    codes = ring_codes(new_key.astype(jnp.bfloat16), encoded_rows)
    codes = codes.astype(jnp.bfloat16)
    normed = batch_norm(codes, bn_gain, bn_shift)
    returned = lax.all_to_all(
        jnp.take(normed, send_back, axis=0), DP, split_axis=0, concat_axis=0, tiled=True
    )
    restored = jnp.take(returned, receive_back, axis=0)
    new_queue = lax.dynamic_update_slice(
        queue, restored[None], (slot[0], jnp.int32(0), jnp.int32(0))
    )
    return (new_params, new_first, new_second, new_key, new_queue)


def solution(mesh):
    groups, dp = mesh.devices.shape
    grid = Mesh(mesh.devices.reshape(groups, dp // 4, 2, 2), ("groups",) + DP)
    rows = P(("groups",) + DP, None)
    in_specs = (
        rows,
        rows,
        rows,
        rows,
        rows,
        rows,
        rows,
        P("groups"),
        P("groups"),
        P("groups"),
        P("groups"),
        P("groups", DP, None),
        P(),
    )
    out_specs = (rows, rows, rows, rows, P("groups", DP, None))
    return jax.shard_map(
        per_device, mesh=grid, in_specs=in_specs, out_specs=out_specs, check_vma=False
    )
```

```python
import jax
import jax.numpy as jnp
from jax import lax
from jax.sharding import Mesh
from jax.sharding import PartitionSpec as P

norm_epsilon = 1e-05
adam_epsilon = 1e-08
bias_first = 1.0 - 0.9**10
bias_second = 1.0 - 0.999**10

DP = ("zo", "xl", "c")


def route(mapping, position, block_rows, per_peer):
    members = mapping.shape[0] // block_rows
    layout = mapping.reshape(members, block_rows)
    owned = layout // block_rows == position
    ordinal = jnp.cumsum(owned.astype(jnp.int32), axis=1) - 1
    offsets = layout - position * block_rows
    slots = jnp.arange(per_peer, dtype=jnp.int32)[None, :, None]
    hit = owned[:, None, :] & (ordinal[:, None, :] == slots)
    send_index = jnp.sum(jnp.where(hit, offsets[:, None, :], 0), axis=2).reshape(-1)
    own_block = lax.dynamic_slice_in_dim(mapping, position * block_rows, block_rows)
    anchor = own_block // block_rows
    indicator = (anchor[:, None] == jnp.arange(members, dtype=jnp.int32)[None, :]).astype(jnp.int32)
    arrival = jnp.sum((jnp.cumsum(indicator, axis=0) - 1) * indicator, axis=1)
    return (send_index, anchor * per_peer + arrival)


def pair_gradient(queries, grad_out):
    tokens, width = queries.shape
    zo = lax.axis_size("zo")
    x = lax.axis_index("xl")
    blocks = queries.reshape(tokens, zo, 2, 2, width // (4 * zo))
    mine = lax.dynamic_index_in_dim(blocks, x, axis=2, keepdims=False)
    theirs = lax.dynamic_index_in_dim(blocks, 1 - x, axis=2, keepdims=False)
    mine = mine.reshape(tokens, width // 2)
    theirs = theirs.reshape(tokens, width // 2)
    swap = [(0, 1), (1, 0)]
    got_queries, got_grad = lax.ppermute((theirs, grad_out), "xl", swap)
    both_queries = jnp.concatenate([mine, got_queries], axis=0)
    both_grad = jnp.concatenate([grad_out, got_grad], axis=0)
    partial = lax.dot_general(
        both_queries, both_grad, (((0,), (0,)), ((), ())), preferred_element_type=jnp.float32
    )
    return lax.psum_scatter(partial, ("zo", "c"), scatter_dimension=0, tiled=True)


def ring_codes(weight, rows):
    zo_size = lax.axis_size("zo")
    length = 2 * zo_size
    block = weight.shape[0]

    def where(q):
        return (q if q < zo_size else length - 1 - q, 0 if q < zo_size else 1)

    def index(zo, xl, c):
        return (zo * 2 + xl) * 2 + c

    def pairs(step):
        return [
            (index(*where(q), c), index(*where((q + step) % length), c))
            for q in range(length)
            for c in (0, 1)
        ]

    forward, backward = pairs(1), pairs(length - 1)
    partner = [
        (index(zo, xl, c), index(zo, xl, 1 - c))
        for zo in range(zo_size)
        for xl in (0, 1)
        for c in (0, 1)
    ]
    zo = lax.axis_index("zo")
    xl = lax.axis_index("xl")
    c = lax.axis_index("c")
    here = jnp.where(xl == 0, zo, length - 1 - zo)

    def columns(offset, cls):
        q = (here + offset) % length
        source = jnp.where(q < zo_size, q, length - 1 - q)
        source = (source * 2 + (q >= zo_size).astype(jnp.int32)) * 2 + cls
        return lax.dynamic_slice_in_dim(rows, source * block, block, axis=1)

    def add(total, offset, cls, shard):
        part = jnp.dot(columns(offset, cls), shard, preferred_element_type=jnp.float32)
        return part if total is None else total + part

    total = add(None, 0, c, weight)
    ahead, behind = weight, weight
    handed = [(0, weight)]
    for step in range(1, length // 2 + 1):
        sent = lax.ppermute(tuple(s for _, s in handed), DP, partner)
        for (offset, _), shard in zip(handed, sent):
            total = add(total, offset, 1 - c, shard)
        handed = []
        ahead = lax.ppermute(ahead, DP, forward)
        total = add(total, -step, c, ahead)
        handed.append((-step, ahead))
        if step < length // 2:
            behind = lax.ppermute(behind, DP, backward)
            total = add(total, step, c, behind)
            handed.append((step, behind))
    sent = lax.ppermute(tuple(s for _, s in handed), DP, partner)
    for (offset, _), shard in zip(handed, sent):
        total = add(total, offset, 1 - c, shard)
    return total


def adamw(gradient, params, first_moment, second_moment, key_params):
    new_first = 0.9 * first_moment + 0.1 * gradient
    new_second = 0.999 * second_moment + 0.001 * gradient * gradient
    update = new_first / bias_first / (jnp.sqrt(new_second / bias_second) + adam_epsilon)
    new_params = params - 0.05 * (update + 0.1 * params)
    new_key = 0.99 * key_params + 0.01 * new_params
    return (new_params, new_first, new_second, new_key)


def per_device(
    queries,
    grad_out,
    params,
    first_moment,
    second_moment,
    key_params,
    keys,
    perm,
    inv_perm,
    bn_gain,
    bn_shift,
    queue,
    slot,
):
    position = lax.axis_index(DP)
    members = lax.axis_size(DP)
    block_rows = keys.shape[0]
    per_peer = block_rows // members
    scaling = 1.0 / jnp.sqrt(jnp.float32(queries.shape[0] * members))
    send_forward, receive_forward = route(perm, position, block_rows, per_peer)
    moved = lax.all_to_all(
        jnp.take(keys, send_forward, axis=0), DP, split_axis=0, concat_axis=0, tiled=True
    )
    encoded_rows = jnp.take(moved, receive_forward, axis=0)
    gradient = pair_gradient(queries, grad_out) * scaling
    gradient, encoded_rows = lax.optimization_barrier((gradient, encoded_rows))
    new_params, new_first, new_second, new_key = adamw(
        gradient, params, first_moment, second_moment, key_params
    )
    codes = ring_codes(
        new_key.astype(jnp.bfloat16), jnp.concatenate([encoded_rows, keys], axis=0)
    ).astype(jnp.bfloat16)
    values = codes[:block_rows].astype(jnp.float32)
    center = jnp.mean(values, axis=0)
    scale = lax.rsqrt(jnp.mean(jnp.square(values - center), axis=0) + norm_epsilon)
    stats = lax.all_gather(jnp.stack([center, scale])[None], DP, axis=0, tiled=True)
    own = lax.dynamic_slice_in_dim(inv_perm, position * block_rows, block_rows)
    stats = jnp.take(stats, own // block_rows, axis=0)
    restored = jax.nn.relu(
        (codes[block_rows:].astype(jnp.float32) - stats[:, 0]) * stats[:, 1] * bn_gain + bn_shift
    ).astype(jnp.bfloat16)
    new_queue = lax.dynamic_update_slice(
        queue, restored[None], (slot[0], jnp.int32(0), jnp.int32(0))
    )
    return (new_params, new_first, new_second, new_key, new_queue)


def solution(mesh):
    groups, dp = mesh.devices.shape
    grid = Mesh(mesh.devices.reshape(groups, dp // 4, 2, 2), ("groups",) + DP)
    rows = P(("groups",) + DP, None)
    in_specs = (
        rows,
        rows,
        rows,
        rows,
        rows,
        rows,
        rows,
        P("groups"),
        P("groups"),
        P("groups"),
        P("groups"),
        P("groups", DP, None),
        P(),
    )
    out_specs = (rows, rows, rows, rows, P("groups", DP, None))
    return jax.shard_map(
        per_device, mesh=grid, in_specs=in_specs, out_specs=out_specs, check_vma=False
    )
```

```python
import jax
import jax.numpy as jnp
from jax import lax
from jax.sharding import Mesh
from jax.sharding import PartitionSpec as P

norm_epsilon = 1e-05
adam_epsilon = 1e-08
bias_first = 1.0 - 0.9**10
bias_second = 1.0 - 0.999**10

DP = ("zo", "xl", "c")


def route(mapping, position, block_rows, per_peer):
    members = mapping.shape[0] // block_rows
    layout = mapping.reshape(members, block_rows)
    owned = layout // block_rows == position
    ordinal = jnp.cumsum(owned.astype(jnp.int32), axis=1) - 1
    offsets = layout - position * block_rows
    slots = jnp.arange(per_peer, dtype=jnp.int32)[None, :, None]
    hit = owned[:, None, :] & (ordinal[:, None, :] == slots)
    send_index = jnp.sum(jnp.where(hit, offsets[:, None, :], 0), axis=2).reshape(-1)
    own_block = lax.dynamic_slice_in_dim(mapping, position * block_rows, block_rows)
    anchor = own_block // block_rows
    indicator = (anchor[:, None] == jnp.arange(members, dtype=jnp.int32)[None, :]).astype(jnp.int32)
    arrival = jnp.sum((jnp.cumsum(indicator, axis=0) - 1) * indicator, axis=1)
    return (send_index, anchor * per_peer + arrival)


def pair_gradient(queries, grad_out):
    tokens, width = queries.shape
    zo = lax.axis_size("zo")
    x = lax.axis_index("xl")
    blocks = queries.reshape(tokens, zo, 2, 2, width // (4 * zo))
    mine = lax.dynamic_index_in_dim(blocks, x, axis=2, keepdims=False)
    theirs = lax.dynamic_index_in_dim(blocks, 1 - x, axis=2, keepdims=False)
    mine = mine.reshape(tokens, width // 2)
    theirs = theirs.reshape(tokens, width // 2)
    swap = [(0, 1), (1, 0)]
    half = grad_out.shape[1] // 2
    got_queries, got_first = lax.ppermute((theirs, grad_out[:, :half]), "xl", swap)
    got_second = lax.ppermute(grad_out[:, half:], "xl", swap)
    both_queries = jnp.concatenate([mine, got_queries], axis=0)
    parts = []
    for own, got in ((grad_out[:, :half], got_first), (grad_out[:, half:], got_second)):
        partial = lax.dot_general(
            both_queries,
            jnp.concatenate([own, got], axis=0),
            (((0,), (0,)), ((), ())),
            preferred_element_type=jnp.float32,
        )
        parts.append(lax.psum_scatter(partial, ("zo", "c"), scatter_dimension=0, tiled=True))
    return parts


def ring_codes(weight, rows):
    zo_size = lax.axis_size("zo")
    length = 2 * zo_size
    block = weight.shape[0]

    def where(q):
        return (q if q < zo_size else length - 1 - q, 0 if q < zo_size else 1)

    def index(zo, xl, c):
        return (zo * 2 + xl) * 2 + c

    def pairs(step):
        return [
            (index(*where(q), c), index(*where((q + step) % length), c))
            for q in range(length)
            for c in (0, 1)
        ]

    forward, backward = pairs(1), pairs(length - 1)
    partner = [
        (index(zo, xl, c), index(zo, xl, 1 - c))
        for zo in range(zo_size)
        for xl in (0, 1)
        for c in (0, 1)
    ]
    zo = lax.axis_index("zo")
    xl = lax.axis_index("xl")
    c = lax.axis_index("c")
    here = jnp.where(xl == 0, zo, length - 1 - zo)

    def columns(offset, cls):
        q = (here + offset) % length
        source = jnp.where(q < zo_size, q, length - 1 - q)
        source = (source * 2 + (q >= zo_size).astype(jnp.int32)) * 2 + cls
        return lax.dynamic_slice_in_dim(rows, source * block, block, axis=1)

    def add(total, offset, cls, shard):
        part = jnp.dot(columns(offset, cls), shard, preferred_element_type=jnp.float32)
        return part if total is None else total + part

    total = add(None, 0, c, weight)
    ahead, behind = weight, weight
    handed = [(0, weight)]
    for step in range(1, length // 2 + 1):
        sent = lax.ppermute(tuple(s for _, s in handed), DP, partner)
        for (offset, _), shard in zip(handed, sent):
            total = add(total, offset, 1 - c, shard)
        handed = []
        ahead = lax.ppermute(ahead, DP, forward)
        total = add(total, -step, c, ahead)
        handed.append((-step, ahead))
        if step < length // 2:
            behind = lax.ppermute(behind, DP, backward)
            total = add(total, step, c, behind)
            handed.append((step, behind))
    sent = lax.ppermute(tuple(s for _, s in handed), DP, partner)
    for (offset, _), shard in zip(handed, sent):
        total = add(total, offset, 1 - c, shard)
    return total


def adamw(gradient, params, first_moment, second_moment, key_params):
    new_first = 0.9 * first_moment + 0.1 * gradient
    new_second = 0.999 * second_moment + 0.001 * gradient * gradient
    update = new_first / bias_first / (jnp.sqrt(new_second / bias_second) + adam_epsilon)
    new_params = params - 0.05 * (update + 0.1 * params)
    new_key = 0.99 * key_params + 0.01 * new_params
    return (new_params, new_first, new_second, new_key)


def batch_norm(codes, bn_gain, bn_shift):
    values = codes.astype(jnp.float32)
    center = jnp.mean(values, axis=0)
    spread = jnp.mean(jnp.square(values - center), axis=0)
    return jax.nn.relu(
        (values - center) * lax.rsqrt(spread + norm_epsilon) * bn_gain + bn_shift
    ).astype(jnp.bfloat16)


def per_device(
    queries,
    grad_out,
    params,
    first_moment,
    second_moment,
    key_params,
    keys,
    perm,
    inv_perm,
    bn_gain,
    bn_shift,
    queue,
    slot,
):
    position = lax.axis_index(DP)
    members = lax.axis_size(DP)
    block_rows = keys.shape[0]
    per_peer = block_rows // members
    scaling = 1.0 / jnp.sqrt(jnp.float32(queries.shape[0] * members))
    send_forward, receive_forward = route(perm, position, block_rows, per_peer)
    send_back, receive_back = route(inv_perm, position, block_rows, per_peer)
    moved = lax.all_to_all(
        jnp.take(keys, send_forward, axis=0), DP, split_axis=0, concat_axis=0, tiled=True
    )
    encoded_rows = jnp.take(moved, receive_forward, axis=0)
    halves = pair_gradient(queries, grad_out)
    halves[0], (encoded_rows, send_back, receive_back) = lax.optimization_barrier(
        (halves[0], (encoded_rows, send_back, receive_back))
    )
    width = params.shape[1] // len(halves)
    results = []
    for h, gradient in enumerate(halves):
        cut = slice(h * width, (h + 1) * width)
        if results:
            gradient, results[-1] = lax.optimization_barrier((gradient, results[-1]))
        updated = adamw(
            gradient * scaling,
            params[:, cut],
            first_moment[:, cut],
            second_moment[:, cut],
            key_params[:, cut],
        )
        codes = ring_codes(updated[3].astype(jnp.bfloat16), encoded_rows)
        normed = batch_norm(codes.astype(jnp.bfloat16), bn_gain[cut], bn_shift[cut])
        returned = lax.all_to_all(
            jnp.take(normed, send_back, axis=0), DP, split_axis=0, concat_axis=0, tiled=True
        )
        results.append(updated + (jnp.take(returned, receive_back, axis=0),))
    new_params, new_first, new_second, new_key, restored = (
        jnp.concatenate(parts, axis=1) for parts in zip(*results)
    )
    new_queue = lax.dynamic_update_slice(
        queue, restored[None], (slot[0], jnp.int32(0), jnp.int32(0))
    )
    return (new_params, new_first, new_second, new_key, new_queue)


def solution(mesh):
    groups, dp = mesh.devices.shape
    grid = Mesh(mesh.devices.reshape(groups, dp // 4, 2, 2), ("groups",) + DP)
    rows = P(("groups",) + DP, None)
    in_specs = (
        rows,
        rows,
        rows,
        rows,
        rows,
        rows,
        rows,
        P("groups"),
        P("groups"),
        P("groups"),
        P("groups"),
        P("groups", DP, None),
        P(),
    )
    out_specs = (rows, rows, rows, rows, P("groups", DP, None))
    return jax.shard_map(
        per_device, mesh=grid, in_specs=in_specs, out_specs=out_specs, check_vma=False
    )
```

```python
import jax
import jax.numpy as jnp
from jax import lax
from jax.sharding import Mesh
from jax.sharding import PartitionSpec as P

norm_epsilon = 1e-05
adam_epsilon = 1e-08
bias_first = 1.0 - 0.9**10
bias_second = 1.0 - 0.999**10

DP = ("zo", "xl", "c")


def route(mapping, position, block_rows, per_peer):
    members = mapping.shape[0] // block_rows
    layout = mapping.reshape(members, block_rows)
    owned = layout // block_rows == position
    ordinal = jnp.cumsum(owned.astype(jnp.int32), axis=1) - 1
    offsets = layout - position * block_rows
    slots = jnp.arange(per_peer, dtype=jnp.int32)[None, :, None]
    hit = owned[:, None, :] & (ordinal[:, None, :] == slots)
    send_index = jnp.sum(jnp.where(hit, offsets[:, None, :], 0), axis=2).reshape(-1)
    own_block = lax.dynamic_slice_in_dim(mapping, position * block_rows, block_rows)
    anchor = own_block // block_rows
    indicator = (anchor[:, None] == jnp.arange(members, dtype=jnp.int32)[None, :]).astype(jnp.int32)
    arrival = jnp.sum((jnp.cumsum(indicator, axis=0) - 1) * indicator, axis=1)
    return (send_index, anchor * per_peer + arrival)


def pair_gradient(queries, grad_out):
    tokens, width = queries.shape
    zo = lax.axis_size("zo")
    c = lax.axis_index("c")
    blocks = queries.reshape(tokens, zo, 2, 2, width // (4 * zo))
    mine = lax.dynamic_index_in_dim(blocks, c, axis=3, keepdims=False)
    theirs = lax.dynamic_index_in_dim(blocks, 1 - c, axis=3, keepdims=False)
    mine = mine.reshape(tokens, width // 2)
    theirs = theirs.reshape(tokens, width // 2)
    swap = [(0, 1), (1, 0)]
    half = grad_out.shape[1] // 2
    got_queries, got_first = lax.ppermute((theirs, grad_out[:, :half]), "c", swap)
    got_second = lax.ppermute(grad_out[:, half:], "c", swap)
    both_queries = jnp.concatenate([mine, got_queries], axis=0)
    parts = []
    for own, got in ((grad_out[:, :half], got_first), (grad_out[:, half:], got_second)):
        partial = lax.dot_general(
            both_queries,
            jnp.concatenate([own, got], axis=0),
            (((0,), (0,)), ((), ())),
            preferred_element_type=jnp.float32,
        )
        parts.append(lax.psum_scatter(partial, ("zo", "xl"), scatter_dimension=0, tiled=True))
    return parts


def ring_codes(weight, rows):
    zo_size = lax.axis_size("zo")
    length = 2 * zo_size
    block = weight.shape[0]

    def where(q):
        return (q if q < zo_size else length - 1 - q, 0 if q < zo_size else 1)

    def index(zo, xl, c):
        return (zo * 2 + xl) * 2 + c

    def pairs(step):
        return [
            (index(*where(q), c), index(*where((q + step) % length), c))
            for q in range(length)
            for c in (0, 1)
        ]

    forward, backward = pairs(1), pairs(length - 1)
    partner = [
        (index(zo, xl, c), index(zo, xl, 1 - c))
        for zo in range(zo_size)
        for xl in (0, 1)
        for c in (0, 1)
    ]
    zo = lax.axis_index("zo")
    xl = lax.axis_index("xl")
    c = lax.axis_index("c")
    here = jnp.where(xl == 0, zo, length - 1 - zo)

    def columns(offset, cls):
        q = (here + offset) % length
        source = jnp.where(q < zo_size, q, length - 1 - q)
        source = (source * 2 + (q >= zo_size).astype(jnp.int32)) * 2 + cls
        return lax.dynamic_slice_in_dim(rows, source * block, block, axis=1)

    def add(total, offset, cls, shard):
        part = jnp.dot(columns(offset, cls), shard, preferred_element_type=jnp.float32)
        return part if total is None else total + part

    total = add(None, 0, c, weight)
    ahead, behind = weight, weight
    handed = [(0, weight)]
    for step in range(1, length // 2 + 1):
        sent = lax.ppermute(tuple(s for _, s in handed), DP, partner)
        for (offset, _), shard in zip(handed, sent):
            total = add(total, offset, 1 - c, shard)
        handed = []
        ahead = lax.ppermute(ahead, DP, forward)
        total = add(total, -step, c, ahead)
        handed.append((-step, ahead))
        if step < length // 2:
            behind = lax.ppermute(behind, DP, backward)
            total = add(total, step, c, behind)
            handed.append((step, behind))
    sent = lax.ppermute(tuple(s for _, s in handed), DP, partner)
    for (offset, _), shard in zip(handed, sent):
        total = add(total, offset, 1 - c, shard)
    return total


def adamw(gradient, params, first_moment, second_moment, key_params):
    new_first = 0.9 * first_moment + 0.1 * gradient
    new_second = 0.999 * second_moment + 0.001 * gradient * gradient
    update = new_first / bias_first / (jnp.sqrt(new_second / bias_second) + adam_epsilon)
    new_params = params - 0.05 * (update + 0.1 * params)
    new_key = 0.99 * key_params + 0.01 * new_params
    return (new_params, new_first, new_second, new_key)


def batch_norm(codes, bn_gain, bn_shift):
    values = codes.astype(jnp.float32)
    center = jnp.mean(values, axis=0)
    spread = jnp.mean(jnp.square(values - center), axis=0)
    return jax.nn.relu(
        (values - center) * lax.rsqrt(spread + norm_epsilon) * bn_gain + bn_shift
    ).astype(jnp.bfloat16)


def per_device(
    queries,
    grad_out,
    params,
    first_moment,
    second_moment,
    key_params,
    keys,
    perm,
    inv_perm,
    bn_gain,
    bn_shift,
    queue,
    slot,
):
    position = lax.axis_index(DP)
    members = lax.axis_size(DP)
    block_rows = keys.shape[0]
    per_peer = block_rows // members
    scaling = 1.0 / jnp.sqrt(jnp.float32(queries.shape[0] * members))
    send_forward, receive_forward = route(perm, position, block_rows, per_peer)
    send_back, receive_back = route(inv_perm, position, block_rows, per_peer)
    moved = lax.all_to_all(
        jnp.take(keys, send_forward, axis=0), DP, split_axis=0, concat_axis=0, tiled=True
    )
    encoded_rows = jnp.take(moved, receive_forward, axis=0)
    halves = pair_gradient(queries, grad_out)
    halves[0], (encoded_rows, send_back, receive_back) = lax.optimization_barrier(
        (halves[0], (encoded_rows, send_back, receive_back))
    )
    width = params.shape[1] // len(halves)
    results = []
    for h, gradient in enumerate(halves):
        cut = slice(h * width, (h + 1) * width)
        if results:
            gradient, results[-1] = lax.optimization_barrier((gradient, results[-1]))
        updated = adamw(
            gradient * scaling,
            params[:, cut],
            first_moment[:, cut],
            second_moment[:, cut],
            key_params[:, cut],
        )
        codes = ring_codes(updated[3].astype(jnp.bfloat16), encoded_rows)
        normed = batch_norm(codes.astype(jnp.bfloat16), bn_gain[cut], bn_shift[cut])
        returned = lax.all_to_all(
            jnp.take(normed, send_back, axis=0), DP, split_axis=0, concat_axis=0, tiled=True
        )
        results.append(updated + (jnp.take(returned, receive_back, axis=0),))
    new_params, new_first, new_second, new_key, restored = (
        jnp.concatenate(parts, axis=1) for parts in zip(*results)
    )
    new_queue = lax.dynamic_update_slice(
        queue, restored[None], (slot[0], jnp.int32(0), jnp.int32(0))
    )
    return (new_params, new_first, new_second, new_key, new_queue)


def solution(mesh):
    groups, dp = mesh.devices.shape
    grid = Mesh(mesh.devices.reshape(groups, dp // 4, 2, 2), ("groups",) + DP)
    rows = P(("groups",) + DP, None)
    in_specs = (
        rows,
        rows,
        rows,
        rows,
        rows,
        rows,
        rows,
        P("groups"),
        P("groups"),
        P("groups"),
        P("groups"),
        P("groups", DP, None),
        P(),
    )
    out_specs = (rows, rows, rows, rows, P("groups", DP, None))
    return jax.shard_map(
        per_device, mesh=grid, in_specs=in_specs, out_specs=out_specs, check_vma=False
    )
```

```python
import jax
import jax.numpy as jnp
from jax import lax
from jax.sharding import Mesh
from jax.sharding import PartitionSpec as P

norm_epsilon = 1e-05
adam_epsilon = 1e-08
bias_first = 1.0 - 0.9**10
bias_second = 1.0 - 0.999**10

DP = ("zo", "xl", "c")


def route(mapping, position, block_rows, per_peer):
    members = mapping.shape[0] // block_rows
    layout = mapping.reshape(members, block_rows)
    owned = layout // block_rows == position
    ordinal = jnp.cumsum(owned.astype(jnp.int32), axis=1) - 1
    offsets = layout - position * block_rows
    slots = jnp.arange(per_peer, dtype=jnp.int32)[None, :, None]
    hit = owned[:, None, :] & (ordinal[:, None, :] == slots)
    send_index = jnp.sum(jnp.where(hit, offsets[:, None, :], 0), axis=2).reshape(-1)
    own_block = lax.dynamic_slice_in_dim(mapping, position * block_rows, block_rows)
    anchor = own_block // block_rows
    indicator = (anchor[:, None] == jnp.arange(members, dtype=jnp.int32)[None, :]).astype(jnp.int32)
    arrival = jnp.sum((jnp.cumsum(indicator, axis=0) - 1) * indicator, axis=1)
    return (send_index, anchor * per_peer + arrival)


def pair_gradient(queries, grad_out):
    tokens, width = queries.shape
    zo = lax.axis_size("zo")
    x = lax.axis_index("xl")
    blocks = queries.reshape(tokens, zo, 2, 2, width // (4 * zo))
    mine = lax.dynamic_index_in_dim(blocks, x, axis=2, keepdims=False)
    theirs = lax.dynamic_index_in_dim(blocks, 1 - x, axis=2, keepdims=False)
    mine = mine.reshape(tokens, width // 2)
    theirs = theirs.reshape(tokens, width // 2)
    swap = [(0, 1), (1, 0)]
    half = grad_out.shape[1] // 2
    got_queries, got_first = lax.ppermute((theirs, grad_out[:, :half]), "xl", swap)
    got_second = lax.ppermute(grad_out[:, half:], "xl", swap)
    both_queries = jnp.concatenate([mine, got_queries], axis=0)
    parts = []
    for own, got in ((grad_out[:, :half], got_first), (grad_out[:, half:], got_second)):
        partial = lax.dot_general(
            both_queries,
            jnp.concatenate([own, got], axis=0),
            (((0,), (0,)), ((), ())),
            preferred_element_type=jnp.float32,
        )
        parts.append(lax.psum_scatter(partial, ("zo", "c"), scatter_dimension=0, tiled=True))
    return parts


def ring_codes(weight, rows):
    zo_size = lax.axis_size("zo")
    length = 2 * zo_size
    block = weight.shape[0]

    def where(q):
        return (q if q < zo_size else length - 1 - q, 0 if q < zo_size else 1)

    def index(zo, xl, c):
        return (zo * 2 + xl) * 2 + c

    def pairs(step):
        return [
            (index(*where(q), c), index(*where((q + step) % length), c))
            for q in range(length)
            for c in (0, 1)
        ]

    forward, backward = pairs(1), pairs(length - 1)
    partner = [
        (index(zo, xl, c), index(zo, xl, 1 - c))
        for zo in range(zo_size)
        for xl in (0, 1)
        for c in (0, 1)
    ]
    zo = lax.axis_index("zo")
    xl = lax.axis_index("xl")
    c = lax.axis_index("c")
    here = jnp.where(xl == 0, zo, length - 1 - zo)

    def columns(offset, cls):
        q = (here + offset) % length
        source = jnp.where(q < zo_size, q, length - 1 - q)
        source = (source * 2 + (q >= zo_size).astype(jnp.int32)) * 2 + cls
        return lax.dynamic_slice_in_dim(rows, source * block, block, axis=1)

    def add(total, offset, cls, shard):
        part = jnp.dot(columns(offset, cls), shard, preferred_element_type=jnp.float32)
        return part if total is None else total + part

    total = add(None, 0, c, weight)
    ahead, behind = weight, weight
    handed = [(0, weight)]
    for step in range(1, length // 2 + 1):
        sent = lax.ppermute(tuple(s for _, s in handed), DP, partner)
        for (offset, _), shard in zip(handed, sent):
            total = add(total, offset, 1 - c, shard)
        handed = []
        ahead = lax.ppermute(ahead, DP, forward)
        total = add(total, -step, c, ahead)
        handed.append((-step, ahead))
        if step < length // 2:
            behind = lax.ppermute(behind, DP, backward)
            total = add(total, step, c, behind)
            handed.append((step, behind))
    sent = lax.ppermute(tuple(s for _, s in handed), DP, partner)
    for (offset, _), shard in zip(handed, sent):
        total = add(total, offset, 1 - c, shard)
    return total


def adamw(gradient, params, first_moment, second_moment, key_params):
    new_first = 0.9 * first_moment + 0.1 * gradient
    new_second = 0.999 * second_moment + 0.001 * gradient * gradient
    update = new_first / bias_first / (jnp.sqrt(new_second / bias_second) + adam_epsilon)
    new_params = params - 0.05 * (update + 0.1 * params)
    new_key = 0.99 * key_params + 0.01 * new_params
    return (new_params, new_first, new_second, new_key)


def batch_norm(codes, bn_gain, bn_shift):
    values = codes.astype(jnp.float32)
    center = jnp.mean(values, axis=0)
    spread = jnp.mean(jnp.square(values - center), axis=0)
    return jax.nn.relu(
        (values - center) * lax.rsqrt(spread + norm_epsilon) * bn_gain + bn_shift
    ).astype(jnp.bfloat16)


def per_device(
    queries,
    grad_out,
    params,
    first_moment,
    second_moment,
    key_params,
    keys,
    perm,
    inv_perm,
    bn_gain,
    bn_shift,
    queue,
    slot,
):
    position = lax.axis_index(DP)
    members = lax.axis_size(DP)
    block_rows = keys.shape[0]
    per_peer = block_rows // members
    scaling = 1.0 / jnp.sqrt(jnp.float32(queries.shape[0] * members))
    send_forward, receive_forward = route(perm, position, block_rows, per_peer)
    send_back, receive_back = route(inv_perm, position, block_rows, per_peer)
    moved = lax.all_to_all(
        jnp.take(keys, send_forward, axis=0), DP, split_axis=0, concat_axis=0, tiled=True
    )
    encoded_rows = jnp.take(moved, receive_forward, axis=0)
    halves = pair_gradient(queries, grad_out)
    halves[0], (encoded_rows, send_back, receive_back) = lax.optimization_barrier(
        (halves[0], (encoded_rows, send_back, receive_back))
    )
    width = params.shape[1] // len(halves)
    results = []
    for h, gradient in enumerate(halves):
        cut = slice(h * width, (h + 1) * width)
        if results:
            gradient, results[-1] = lax.optimization_barrier((gradient, results[-1]))
        updated = adamw(
            gradient * scaling,
            params[:, cut],
            first_moment[:, cut],
            second_moment[:, cut],
            key_params[:, cut],
        )
        codes = ring_codes(updated[3].astype(jnp.bfloat16), encoded_rows)
        normed = batch_norm(codes.astype(jnp.bfloat16), bn_gain[cut], bn_shift[cut])
        results.append(updated + (normed,))
    new_params, new_first, new_second, new_key, normed = (
        jnp.concatenate(parts, axis=1) for parts in zip(*results)
    )
    returned = lax.all_to_all(
        jnp.take(normed, send_back, axis=0), DP, split_axis=0, concat_axis=0, tiled=True
    )
    restored = jnp.take(returned, receive_back, axis=0)
    new_queue = lax.dynamic_update_slice(
        queue, restored[None], (slot[0], jnp.int32(0), jnp.int32(0))
    )
    return (new_params, new_first, new_second, new_key, new_queue)


def solution(mesh):
    groups, dp = mesh.devices.shape
    grid = Mesh(mesh.devices.reshape(groups, dp // 4, 2, 2), ("groups",) + DP)
    rows = P(("groups",) + DP, None)
    in_specs = (
        rows,
        rows,
        rows,
        rows,
        rows,
        rows,
        rows,
        P("groups"),
        P("groups"),
        P("groups"),
        P("groups"),
        P("groups", DP, None),
        P(),
    )
    out_specs = (rows, rows, rows, rows, P("groups", DP, None))
    return jax.shard_map(
        per_device, mesh=grid, in_specs=in_specs, out_specs=out_specs, check_vma=False
    )
```

```python
import jax
import jax.numpy as jnp
from jax import lax
from jax.sharding import Mesh
from jax.sharding import PartitionSpec as P

norm_epsilon = 1e-05
adam_epsilon = 1e-08
bias_first = 1.0 - 0.9**10
bias_second = 1.0 - 0.999**10

DP = ("zo", "xl", "c")


def route(mapping, position, block_rows, per_peer):
    members = mapping.shape[0] // block_rows
    layout = mapping.reshape(members, block_rows)
    owned = layout // block_rows == position
    ordinal = jnp.cumsum(owned.astype(jnp.int32), axis=1) - 1
    offsets = layout - position * block_rows
    slots = jnp.arange(per_peer, dtype=jnp.int32)[None, :, None]
    hit = owned[:, None, :] & (ordinal[:, None, :] == slots)
    send_index = jnp.sum(jnp.where(hit, offsets[:, None, :], 0), axis=2).reshape(-1)
    own_block = lax.dynamic_slice_in_dim(mapping, position * block_rows, block_rows)
    anchor = own_block // block_rows
    indicator = (anchor[:, None] == jnp.arange(members, dtype=jnp.int32)[None, :]).astype(jnp.int32)
    arrival = jnp.sum((jnp.cumsum(indicator, axis=0) - 1) * indicator, axis=1)
    return (send_index, anchor * per_peer + arrival)


def pair_gradient(queries, grad_out):
    tokens, width = queries.shape
    zo = lax.axis_size("zo")
    x = lax.axis_index("xl")
    blocks = queries.reshape(tokens, zo, 2, 2, width // (4 * zo))
    mine = lax.dynamic_index_in_dim(blocks, x, axis=2, keepdims=False)
    theirs = lax.dynamic_index_in_dim(blocks, 1 - x, axis=2, keepdims=False)
    mine = mine.reshape(tokens, width // 2)
    theirs = theirs.reshape(tokens, width // 2)
    swap = [(0, 1), (1, 0)]
    half = grad_out.shape[1] // 2
    got_queries, got_first = lax.ppermute((theirs, grad_out[:, :half]), "xl", swap)
    got_second = lax.ppermute(grad_out[:, half:], "xl", swap)
    both_queries = jnp.concatenate([mine, got_queries], axis=0)
    parts = []
    for own, got in ((grad_out[:, :half], got_first), (grad_out[:, half:], got_second)):
        partial = lax.dot_general(
            both_queries,
            jnp.concatenate([own, got], axis=0),
            (((0,), (0,)), ((), ())),
            preferred_element_type=jnp.float32,
        )
        parts.append(lax.psum_scatter(partial, ("zo", "c"), scatter_dimension=0, tiled=True))
    return parts


def ring_codes(weight, rows):
    zo_size = lax.axis_size("zo")
    length = 2 * zo_size
    block = weight.shape[0]

    def where(q):
        return (q if q < zo_size else length - 1 - q, 0 if q < zo_size else 1)

    def index(zo, xl, c):
        return (zo * 2 + xl) * 2 + c

    def pairs(step):
        return [
            (index(*where(q), c), index(*where((q + step) % length), c))
            for q in range(length)
            for c in (0, 1)
        ]

    forward, backward = pairs(1), pairs(length - 1)
    partner = [
        (index(zo, xl, c), index(zo, xl, 1 - c))
        for zo in range(zo_size)
        for xl in (0, 1)
        for c in (0, 1)
    ]
    zo = lax.axis_index("zo")
    xl = lax.axis_index("xl")
    c = lax.axis_index("c")
    here = jnp.where(xl == 0, zo, length - 1 - zo)

    def columns(offset, cls):
        q = (here + offset) % length
        source = jnp.where(q < zo_size, q, length - 1 - q)
        source = (source * 2 + (q >= zo_size).astype(jnp.int32)) * 2 + cls
        return lax.dynamic_slice_in_dim(rows, source * block, block, axis=1)

    def add(total, offset, cls, shard):
        part = jnp.dot(columns(offset, cls), shard, preferred_element_type=jnp.float32)
        return part if total is None else total + part

    total = add(None, 0, c, weight)
    ahead, behind = weight, weight
    handed = [(0, weight)]
    for step in range(1, length // 2 + 1):
        sent = lax.ppermute(tuple(s for _, s in handed), DP, partner)
        for (offset, _), shard in zip(handed, sent):
            total = add(total, offset, 1 - c, shard)
        handed = []
        ahead = lax.ppermute(ahead, DP, forward)
        total = add(total, -step, c, ahead)
        handed.append((-step, ahead))
        if step < length // 2:
            behind = lax.ppermute(behind, DP, backward)
            total = add(total, step, c, behind)
            handed.append((step, behind))
    sent = lax.ppermute(tuple(s for _, s in handed), DP, partner)
    for (offset, _), shard in zip(handed, sent):
        total = add(total, offset, 1 - c, shard)
    return total


def adamw(gradient, params, first_moment, second_moment, key_params):
    new_first = 0.9 * first_moment + 0.1 * gradient
    new_second = 0.999 * second_moment + 0.001 * gradient * gradient
    update = new_first / bias_first / (jnp.sqrt(new_second / bias_second) + adam_epsilon)
    new_params = params - 0.05 * (update + 0.1 * params)
    new_key = 0.99 * key_params + 0.01 * new_params
    return (new_params, new_first, new_second, new_key)


def batch_norm(codes, bn_gain, bn_shift):
    values = codes.astype(jnp.float32)
    center = jnp.mean(values, axis=0)
    spread = jnp.mean(jnp.square(values - center), axis=0)
    return jax.nn.relu(
        (values - center) * lax.rsqrt(spread + norm_epsilon) * bn_gain + bn_shift
    ).astype(jnp.bfloat16)


def per_device(
    queries,
    grad_out,
    params,
    first_moment,
    second_moment,
    key_params,
    keys,
    perm,
    inv_perm,
    bn_gain,
    bn_shift,
    queue,
    slot,
):
    position = lax.axis_index(DP)
    members = lax.axis_size(DP)
    block_rows = keys.shape[0]
    per_peer = block_rows // members
    scaling = 1.0 / jnp.sqrt(jnp.float32(queries.shape[0] * members))
    send_forward, receive_forward = route(perm, position, block_rows, per_peer)
    send_back, receive_back = route(inv_perm, position, block_rows, per_peer)
    moved = lax.all_to_all(
        jnp.take(keys, send_forward, axis=0), DP, split_axis=0, concat_axis=0, tiled=True
    )
    encoded_rows = jnp.take(moved, receive_forward, axis=0)
    halves = pair_gradient(queries, grad_out)
    halves[0], (encoded_rows, send_back, receive_back) = lax.optimization_barrier(
        (halves[0], (encoded_rows, send_back, receive_back))
    )
    kept = encoded_rows[0, 0] == encoded_rows[0, 0]
    queue = lax.optimization_barrier(jnp.where(kept, queue, jnp.zeros_like(queue)))
    width = params.shape[1] // len(halves)
    results = []
    for h, gradient in enumerate(halves):
        cut = slice(h * width, (h + 1) * width)
        if results:
            gradient, results[-1] = lax.optimization_barrier((gradient, results[-1]))
        updated = adamw(
            gradient * scaling,
            params[:, cut],
            first_moment[:, cut],
            second_moment[:, cut],
            key_params[:, cut],
        )
        codes = ring_codes(updated[3].astype(jnp.bfloat16), encoded_rows)
        normed = batch_norm(codes.astype(jnp.bfloat16), bn_gain[cut], bn_shift[cut])
        results.append(updated + (normed,))
    new_params, new_first, new_second, new_key, normed = (
        jnp.concatenate(parts, axis=1) for parts in zip(*results)
    )
    returned = lax.all_to_all(
        jnp.take(normed, send_back, axis=0), DP, split_axis=0, concat_axis=0, tiled=True
    )
    restored = jnp.take(returned, receive_back, axis=0)
    new_queue = lax.dynamic_update_slice(
        queue, restored[None], (slot[0], jnp.int32(0), jnp.int32(0))
    )
    return (new_params, new_first, new_second, new_key, new_queue)


def solution(mesh):
    groups, dp = mesh.devices.shape
    grid = Mesh(mesh.devices.reshape(groups, dp // 4, 2, 2), ("groups",) + DP)
    rows = P(("groups",) + DP, None)
    in_specs = (
        rows,
        rows,
        rows,
        rows,
        rows,
        rows,
        rows,
        P("groups"),
        P("groups"),
        P("groups"),
        P("groups"),
        P("groups", DP, None),
        P(),
    )
    out_specs = (rows, rows, rows, rows, P("groups", DP, None))
    return jax.shard_map(
        per_device, mesh=grid, in_specs=in_specs, out_specs=out_specs, check_vma=False
    )
```

```python
import jax
import jax.numpy as jnp
from jax import lax
from jax.sharding import Mesh
from jax.sharding import PartitionSpec as P

norm_epsilon = 1e-05
adam_epsilon = 1e-08
bias_first = 1.0 - 0.9**10
bias_second = 1.0 - 0.999**10

DP = ("zo", "xl", "c")


def route(mapping, position, block_rows, per_peer):
    members = mapping.shape[0] // block_rows
    layout = mapping.reshape(members, block_rows)
    owned = layout // block_rows == position
    ordinal = jnp.cumsum(owned.astype(jnp.int32), axis=1) - 1
    offsets = layout - position * block_rows
    slots = jnp.arange(per_peer, dtype=jnp.int32)[None, :, None]
    hit = owned[:, None, :] & (ordinal[:, None, :] == slots)
    send_index = jnp.sum(jnp.where(hit, offsets[:, None, :], 0), axis=2).reshape(-1)
    own_block = lax.dynamic_slice_in_dim(mapping, position * block_rows, block_rows)
    anchor = own_block // block_rows
    indicator = (anchor[:, None] == jnp.arange(members, dtype=jnp.int32)[None, :]).astype(jnp.int32)
    arrival = jnp.sum((jnp.cumsum(indicator, axis=0) - 1) * indicator, axis=1)
    return (send_index, anchor * per_peer + arrival)


def pair_gradient(queries, grad_out):
    tokens, width = queries.shape
    zo = lax.axis_size("zo")
    x = lax.axis_index("xl")
    blocks = queries.reshape(tokens, zo, 2, 2, width // (4 * zo))
    mine = lax.dynamic_index_in_dim(blocks, x, axis=2, keepdims=False)
    theirs = lax.dynamic_index_in_dim(blocks, 1 - x, axis=2, keepdims=False)
    mine = mine.reshape(tokens, width // 2)
    theirs = theirs.reshape(tokens, width // 2)
    swap = [(0, 1), (1, 0)]
    half = grad_out.shape[1] // 2
    got_queries, got_first = lax.ppermute((theirs, grad_out[:, :half]), "xl", swap)
    got_second = lax.ppermute(grad_out[:, half:], "xl", swap)
    parts = []
    for own, got in ((grad_out[:, :half], got_first), (grad_out[:, half:], got_second)):
        partial = lax.dot_general(
            mine, own, (((0,), (0,)), ((), ())), preferred_element_type=jnp.float32
        ) + lax.dot_general(
            got_queries, got, (((0,), (0,)), ((), ())), preferred_element_type=jnp.float32
        )
        parts.append(lax.psum_scatter(partial, ("zo", "c"), scatter_dimension=0, tiled=True))
    return parts


def ring_codes(weight, rows):
    zo_size = lax.axis_size("zo")
    length = 2 * zo_size
    block = weight.shape[0]

    def where(q):
        return (q if q < zo_size else length - 1 - q, 0 if q < zo_size else 1)

    def index(zo, xl, c):
        return (zo * 2 + xl) * 2 + c

    def pairs(step):
        return [
            (index(*where(q), c), index(*where((q + step) % length), c))
            for q in range(length)
            for c in (0, 1)
        ]

    forward, backward = pairs(1), pairs(length - 1)
    partner = [
        (index(zo, xl, c), index(zo, xl, 1 - c))
        for zo in range(zo_size)
        for xl in (0, 1)
        for c in (0, 1)
    ]
    zo = lax.axis_index("zo")
    xl = lax.axis_index("xl")
    c = lax.axis_index("c")
    here = jnp.where(xl == 0, zo, length - 1 - zo)

    def columns(offset, cls):
        q = (here + offset) % length
        source = jnp.where(q < zo_size, q, length - 1 - q)
        source = (source * 2 + (q >= zo_size).astype(jnp.int32)) * 2 + cls
        return lax.dynamic_slice_in_dim(rows, source * block, block, axis=1)

    def add(total, offset, cls, shard):
        part = jnp.dot(columns(offset, cls), shard, preferred_element_type=jnp.float32)
        return part if total is None else total + part

    total = add(None, 0, c, weight)
    ahead, behind = weight, weight
    handed = [(0, weight)]
    for step in range(1, length // 2 + 1):
        sent = lax.ppermute(tuple(s for _, s in handed), DP, partner)
        for (offset, _), shard in zip(handed, sent):
            total = add(total, offset, 1 - c, shard)
        handed = []
        ahead = lax.ppermute(ahead, DP, forward)
        total = add(total, -step, c, ahead)
        handed.append((-step, ahead))
        if step < length // 2:
            behind = lax.ppermute(behind, DP, backward)
            total = add(total, step, c, behind)
            handed.append((step, behind))
    sent = lax.ppermute(tuple(s for _, s in handed), DP, partner)
    for (offset, _), shard in zip(handed, sent):
        total = add(total, offset, 1 - c, shard)
    return total


def adamw(gradient, params, first_moment, second_moment, key_params):
    new_first = 0.9 * first_moment + 0.1 * gradient
    new_second = 0.999 * second_moment + 0.001 * gradient * gradient
    update = new_first / bias_first / (jnp.sqrt(new_second / bias_second) + adam_epsilon)
    new_params = params - 0.05 * (update + 0.1 * params)
    new_key = 0.99 * key_params + 0.01 * new_params
    return (new_params, new_first, new_second, new_key)


def batch_norm(codes, bn_gain, bn_shift):
    values = codes.astype(jnp.float32)
    center = jnp.mean(values, axis=0)
    spread = jnp.mean(jnp.square(values - center), axis=0)
    return jax.nn.relu(
        (values - center) * lax.rsqrt(spread + norm_epsilon) * bn_gain + bn_shift
    ).astype(jnp.bfloat16)


def per_device(
    queries,
    grad_out,
    params,
    first_moment,
    second_moment,
    key_params,
    keys,
    perm,
    inv_perm,
    bn_gain,
    bn_shift,
    queue,
    slot,
):
    position = lax.axis_index(DP)
    members = lax.axis_size(DP)
    block_rows = keys.shape[0]
    per_peer = block_rows // members
    scaling = 1.0 / jnp.sqrt(jnp.float32(queries.shape[0] * members))
    send_forward, receive_forward = route(perm, position, block_rows, per_peer)
    send_back, receive_back = route(inv_perm, position, block_rows, per_peer)
    moved = lax.all_to_all(
        jnp.take(keys, send_forward, axis=0), DP, split_axis=0, concat_axis=0, tiled=True
    )
    encoded_rows = jnp.take(moved, receive_forward, axis=0)
    halves = pair_gradient(queries, grad_out)
    halves[0], (encoded_rows, send_back, receive_back) = lax.optimization_barrier(
        (halves[0], (encoded_rows, send_back, receive_back))
    )
    kept = encoded_rows[0, 0] == encoded_rows[0, 0]
    queue = lax.optimization_barrier(jnp.where(kept, queue, jnp.zeros_like(queue)))
    width = params.shape[1] // len(halves)
    results = []
    for h, gradient in enumerate(halves):
        cut = slice(h * width, (h + 1) * width)
        if results:
            gradient, results[-1] = lax.optimization_barrier((gradient, results[-1]))
        updated = adamw(
            gradient * scaling,
            params[:, cut],
            first_moment[:, cut],
            second_moment[:, cut],
            key_params[:, cut],
        )
        codes = ring_codes(updated[3].astype(jnp.bfloat16), encoded_rows)
        normed = batch_norm(codes.astype(jnp.bfloat16), bn_gain[cut], bn_shift[cut])
        results.append(updated + (normed,))
    new_params, new_first, new_second, new_key, normed = (
        jnp.concatenate(parts, axis=1) for parts in zip(*results)
    )
    returned = lax.all_to_all(
        jnp.take(normed, send_back, axis=0), DP, split_axis=0, concat_axis=0, tiled=True
    )
    restored = jnp.take(returned, receive_back, axis=0)
    new_queue = lax.dynamic_update_slice(
        queue, restored[None], (slot[0], jnp.int32(0), jnp.int32(0))
    )
    return (new_params, new_first, new_second, new_key, new_queue)


def solution(mesh):
    groups, dp = mesh.devices.shape
    grid = Mesh(mesh.devices.reshape(groups, dp // 4, 2, 2), ("groups",) + DP)
    rows = P(("groups",) + DP, None)
    in_specs = (
        rows,
        rows,
        rows,
        rows,
        rows,
        rows,
        rows,
        P("groups"),
        P("groups"),
        P("groups"),
        P("groups"),
        P("groups", DP, None),
        P(),
    )
    out_specs = (rows, rows, rows, rows, P("groups", DP, None))
    return jax.shard_map(
        per_device, mesh=grid, in_specs=in_specs, out_specs=out_specs, check_vma=False
    )
```

```python
import jax
import jax.numpy as jnp
from jax import lax
from jax.sharding import Mesh
from jax.sharding import PartitionSpec as P

norm_epsilon = 1e-05
adam_epsilon = 1e-08
bias_first = 1.0 - 0.9**10
bias_second = 1.0 - 0.999**10

DP = ("zo", "xl", "c")


def route(mapping, position, block_rows, per_peer):
    members = mapping.shape[0] // block_rows
    layout = mapping.reshape(members, block_rows)
    owned = layout // block_rows == position
    ordinal = jnp.cumsum(owned.astype(jnp.int32), axis=1) - 1
    offsets = layout - position * block_rows
    slots = jnp.arange(per_peer, dtype=jnp.int32)[None, :, None]
    hit = owned[:, None, :] & (ordinal[:, None, :] == slots)
    send_index = jnp.sum(jnp.where(hit, offsets[:, None, :], 0), axis=2).reshape(-1)
    own_block = lax.dynamic_slice_in_dim(mapping, position * block_rows, block_rows)
    anchor = own_block // block_rows
    indicator = (anchor[:, None] == jnp.arange(members, dtype=jnp.int32)[None, :]).astype(jnp.int32)
    arrival = jnp.sum((jnp.cumsum(indicator, axis=0) - 1) * indicator, axis=1)
    return (send_index, anchor * per_peer + arrival)


def pair_gradient(queries, grad_out):
    tokens, width = queries.shape
    zo = lax.axis_size("zo")
    x = lax.axis_index("xl")
    blocks = queries.reshape(tokens, zo, 2, 2, width // (4 * zo))
    mine = lax.dynamic_index_in_dim(blocks, x, axis=2, keepdims=False)
    theirs = lax.dynamic_index_in_dim(blocks, 1 - x, axis=2, keepdims=False)
    mine = mine.reshape(tokens, width // 2)
    theirs = theirs.reshape(tokens, width // 2)
    swap = [(0, 1), (1, 0)]
    half = grad_out.shape[1] * 9 // 16
    got_queries, got_first = lax.ppermute((theirs, grad_out[:, :half]), "xl", swap)
    got_second = lax.ppermute(grad_out[:, half:], "xl", swap)
    both_queries = jnp.concatenate([mine, got_queries], axis=0)
    parts = []
    for own, got in ((grad_out[:, :half], got_first), (grad_out[:, half:], got_second)):
        partial = lax.dot_general(
            both_queries,
            jnp.concatenate([own, got], axis=0),
            (((0,), (0,)), ((), ())),
            preferred_element_type=jnp.float32,
        )
        parts.append(lax.psum_scatter(partial, ("zo", "c"), scatter_dimension=0, tiled=True))
    return parts


def ring_codes(weight, rows):
    zo_size = lax.axis_size("zo")
    length = 2 * zo_size
    block = weight.shape[0]

    def where(q):
        return (q if q < zo_size else length - 1 - q, 0 if q < zo_size else 1)

    def index(zo, xl, c):
        return (zo * 2 + xl) * 2 + c

    def pairs(step):
        return [
            (index(*where(q), c), index(*where((q + step) % length), c))
            for q in range(length)
            for c in (0, 1)
        ]

    forward, backward = pairs(1), pairs(length - 1)
    partner = [
        (index(zo, xl, c), index(zo, xl, 1 - c))
        for zo in range(zo_size)
        for xl in (0, 1)
        for c in (0, 1)
    ]
    zo = lax.axis_index("zo")
    xl = lax.axis_index("xl")
    c = lax.axis_index("c")
    here = jnp.where(xl == 0, zo, length - 1 - zo)

    def columns(offset, cls):
        q = (here + offset) % length
        source = jnp.where(q < zo_size, q, length - 1 - q)
        source = (source * 2 + (q >= zo_size).astype(jnp.int32)) * 2 + cls
        return lax.dynamic_slice_in_dim(rows, source * block, block, axis=1)

    def add(total, offset, cls, shard):
        part = jnp.dot(columns(offset, cls), shard, preferred_element_type=jnp.float32)
        return part if total is None else total + part

    total = add(None, 0, c, weight)
    ahead, behind = weight, weight
    handed = [(0, weight)]
    for step in range(1, length // 2 + 1):
        sent = lax.ppermute(tuple(s for _, s in handed), DP, partner)
        for (offset, _), shard in zip(handed, sent):
            total = add(total, offset, 1 - c, shard)
        handed = []
        ahead = lax.ppermute(ahead, DP, forward)
        total = add(total, -step, c, ahead)
        handed.append((-step, ahead))
        if step < length // 2:
            behind = lax.ppermute(behind, DP, backward)
            total = add(total, step, c, behind)
            handed.append((step, behind))
    sent = lax.ppermute(tuple(s for _, s in handed), DP, partner)
    for (offset, _), shard in zip(handed, sent):
        total = add(total, offset, 1 - c, shard)
    return total


def adamw(gradient, params, first_moment, second_moment, key_params):
    new_first = 0.9 * first_moment + 0.1 * gradient
    new_second = 0.999 * second_moment + 0.001 * gradient * gradient
    update = new_first / bias_first / (jnp.sqrt(new_second / bias_second) + adam_epsilon)
    new_params = params - 0.05 * (update + 0.1 * params)
    new_key = 0.99 * key_params + 0.01 * new_params
    return (new_params, new_first, new_second, new_key)


def batch_norm(codes, bn_gain, bn_shift):
    values = codes.astype(jnp.float32)
    center = jnp.mean(values, axis=0)
    spread = jnp.mean(jnp.square(values - center), axis=0)
    return jax.nn.relu(
        (values - center) * lax.rsqrt(spread + norm_epsilon) * bn_gain + bn_shift
    ).astype(jnp.bfloat16)


def per_device(
    queries,
    grad_out,
    params,
    first_moment,
    second_moment,
    key_params,
    keys,
    perm,
    inv_perm,
    bn_gain,
    bn_shift,
    queue,
    slot,
):
    position = lax.axis_index(DP)
    members = lax.axis_size(DP)
    block_rows = keys.shape[0]
    per_peer = block_rows // members
    scaling = 1.0 / jnp.sqrt(jnp.float32(queries.shape[0] * members))
    send_forward, receive_forward = route(perm, position, block_rows, per_peer)
    send_back, receive_back = route(inv_perm, position, block_rows, per_peer)
    moved = lax.all_to_all(
        jnp.take(keys, send_forward, axis=0), DP, split_axis=0, concat_axis=0, tiled=True
    )
    encoded_rows = jnp.take(moved, receive_forward, axis=0)
    halves = pair_gradient(queries, grad_out)
    halves[0], (encoded_rows, send_back, receive_back) = lax.optimization_barrier(
        (halves[0], (encoded_rows, send_back, receive_back))
    )
    kept = encoded_rows[0, 0] == encoded_rows[0, 0]
    queue = lax.optimization_barrier(jnp.where(kept, queue, jnp.zeros_like(queue)))
    results = []
    start = 0
    for gradient in halves:
        cut = slice(start, start + gradient.shape[1])
        start += gradient.shape[1]
        if results:
            gradient, results[-1] = lax.optimization_barrier((gradient, results[-1]))
        updated = adamw(
            gradient * scaling,
            params[:, cut],
            first_moment[:, cut],
            second_moment[:, cut],
            key_params[:, cut],
        )
        codes = ring_codes(updated[3].astype(jnp.bfloat16), encoded_rows)
        normed = batch_norm(codes.astype(jnp.bfloat16), bn_gain[cut], bn_shift[cut])
        results.append(updated + (normed,))
    new_params, new_first, new_second, new_key, normed = (
        jnp.concatenate(parts, axis=1) for parts in zip(*results)
    )
    returned = lax.all_to_all(
        jnp.take(normed, send_back, axis=0), DP, split_axis=0, concat_axis=0, tiled=True
    )
    restored = jnp.take(returned, receive_back, axis=0)
    new_queue = lax.dynamic_update_slice(
        queue, restored[None], (slot[0], jnp.int32(0), jnp.int32(0))
    )
    return (new_params, new_first, new_second, new_key, new_queue)


def solution(mesh):
    groups, dp = mesh.devices.shape
    grid = Mesh(mesh.devices.reshape(groups, dp // 4, 2, 2), ("groups",) + DP)
    rows = P(("groups",) + DP, None)
    in_specs = (
        rows,
        rows,
        rows,
        rows,
        rows,
        rows,
        rows,
        P("groups"),
        P("groups"),
        P("groups"),
        P("groups"),
        P("groups", DP, None),
        P(),
    )
    out_specs = (rows, rows, rows, rows, P("groups", DP, None))
    return jax.shard_map(
        per_device, mesh=grid, in_specs=in_specs, out_specs=out_specs, check_vma=False
    )
```

```python
import jax
import jax.numpy as jnp
from jax import lax
from jax.sharding import Mesh
from jax.sharding import PartitionSpec as P

norm_epsilon = 1e-05
adam_epsilon = 1e-08
bias_first = 1.0 - 0.9**10
bias_second = 1.0 - 0.999**10

DP = ("zo", "xl", "c")


def route(mapping, position, block_rows, per_peer):
    members = mapping.shape[0] // block_rows
    layout = mapping.reshape(members, block_rows)
    owned = layout // block_rows == position
    ordinal = jnp.cumsum(owned.astype(jnp.int32), axis=1) - 1
    offsets = layout - position * block_rows
    slots = jnp.arange(per_peer, dtype=jnp.int32)[None, :, None]
    hit = owned[:, None, :] & (ordinal[:, None, :] == slots)
    send_index = jnp.sum(jnp.where(hit, offsets[:, None, :], 0), axis=2).reshape(-1)
    own_block = lax.dynamic_slice_in_dim(mapping, position * block_rows, block_rows)
    anchor = own_block // block_rows
    indicator = (anchor[:, None] == jnp.arange(members, dtype=jnp.int32)[None, :]).astype(jnp.int32)
    arrival = jnp.sum((jnp.cumsum(indicator, axis=0) - 1) * indicator, axis=1)
    return (send_index, anchor * per_peer + arrival)


def pair_gradient(queries, grad_out):
    tokens, width = queries.shape
    zo = lax.axis_size("zo")
    x = lax.axis_index("xl")
    blocks = queries.reshape(tokens, zo, 2, 2, width // (4 * zo))
    mine = lax.dynamic_index_in_dim(blocks, x, axis=2, keepdims=False)
    theirs = lax.dynamic_index_in_dim(blocks, 1 - x, axis=2, keepdims=False)
    mine = mine.reshape(tokens, width // 2)
    theirs = theirs.reshape(tokens, width // 2)
    swap = [(0, 1), (1, 0)]
    half = grad_out.shape[1] * 7 // 16
    got_queries, got_first = lax.ppermute((theirs, grad_out[:, :half]), "xl", swap)
    got_second = lax.ppermute(grad_out[:, half:], "xl", swap)
    both_queries = jnp.concatenate([mine, got_queries], axis=0)
    parts = []
    for own, got in ((grad_out[:, :half], got_first), (grad_out[:, half:], got_second)):
        partial = lax.dot_general(
            both_queries,
            jnp.concatenate([own, got], axis=0),
            (((0,), (0,)), ((), ())),
            preferred_element_type=jnp.float32,
        )
        parts.append(lax.psum_scatter(partial, ("zo", "c"), scatter_dimension=0, tiled=True))
    return parts


def ring_codes(weight, rows):
    zo_size = lax.axis_size("zo")
    length = 2 * zo_size
    block = weight.shape[0]

    def where(q):
        return (q if q < zo_size else length - 1 - q, 0 if q < zo_size else 1)

    def index(zo, xl, c):
        return (zo * 2 + xl) * 2 + c

    def pairs(step):
        return [
            (index(*where(q), c), index(*where((q + step) % length), c))
            for q in range(length)
            for c in (0, 1)
        ]

    forward, backward = pairs(1), pairs(length - 1)
    partner = [
        (index(zo, xl, c), index(zo, xl, 1 - c))
        for zo in range(zo_size)
        for xl in (0, 1)
        for c in (0, 1)
    ]
    zo = lax.axis_index("zo")
    xl = lax.axis_index("xl")
    c = lax.axis_index("c")
    here = jnp.where(xl == 0, zo, length - 1 - zo)

    def columns(offset, cls):
        q = (here + offset) % length
        source = jnp.where(q < zo_size, q, length - 1 - q)
        source = (source * 2 + (q >= zo_size).astype(jnp.int32)) * 2 + cls
        return lax.dynamic_slice_in_dim(rows, source * block, block, axis=1)

    def add(total, offset, cls, shard):
        part = jnp.dot(columns(offset, cls), shard, preferred_element_type=jnp.float32)
        return part if total is None else total + part

    total = add(None, 0, c, weight)
    ahead, behind = weight, weight
    handed = [(0, weight)]
    for step in range(1, length // 2 + 1):
        sent = lax.ppermute(tuple(s for _, s in handed), DP, partner)
        for (offset, _), shard in zip(handed, sent):
            total = add(total, offset, 1 - c, shard)
        handed = []
        ahead = lax.ppermute(ahead, DP, forward)
        total = add(total, -step, c, ahead)
        handed.append((-step, ahead))
        if step < length // 2:
            behind = lax.ppermute(behind, DP, backward)
            total = add(total, step, c, behind)
            handed.append((step, behind))
    sent = lax.ppermute(tuple(s for _, s in handed), DP, partner)
    for (offset, _), shard in zip(handed, sent):
        total = add(total, offset, 1 - c, shard)
    return total


def adamw(gradient, params, first_moment, second_moment, key_params):
    new_first = 0.9 * first_moment + 0.1 * gradient
    new_second = 0.999 * second_moment + 0.001 * gradient * gradient
    update = new_first / bias_first / (jnp.sqrt(new_second / bias_second) + adam_epsilon)
    new_params = params - 0.05 * (update + 0.1 * params)
    new_key = 0.99 * key_params + 0.01 * new_params
    return (new_params, new_first, new_second, new_key)


def batch_norm(codes, bn_gain, bn_shift):
    values = codes.astype(jnp.float32)
    center = jnp.mean(values, axis=0)
    spread = jnp.mean(jnp.square(values - center), axis=0)
    return jax.nn.relu(
        (values - center) * lax.rsqrt(spread + norm_epsilon) * bn_gain + bn_shift
    ).astype(jnp.bfloat16)


def per_device(
    queries,
    grad_out,
    params,
    first_moment,
    second_moment,
    key_params,
    keys,
    perm,
    inv_perm,
    bn_gain,
    bn_shift,
    queue,
    slot,
):
    position = lax.axis_index(DP)
    members = lax.axis_size(DP)
    block_rows = keys.shape[0]
    per_peer = block_rows // members
    scaling = 1.0 / jnp.sqrt(jnp.float32(queries.shape[0] * members))
    send_forward, receive_forward = route(perm, position, block_rows, per_peer)
    send_back, receive_back = route(inv_perm, position, block_rows, per_peer)
    moved = lax.all_to_all(
        jnp.take(keys, send_forward, axis=0), DP, split_axis=0, concat_axis=0, tiled=True
    )
    encoded_rows = jnp.take(moved, receive_forward, axis=0)
    halves = pair_gradient(queries, grad_out)
    halves[0], (encoded_rows, send_back, receive_back) = lax.optimization_barrier(
        (halves[0], (encoded_rows, send_back, receive_back))
    )
    kept = encoded_rows[0, 0] == encoded_rows[0, 0]
    queue = lax.optimization_barrier(jnp.where(kept, queue, jnp.zeros_like(queue)))
    results = []
    start = 0
    for gradient in halves:
        cut = slice(start, start + gradient.shape[1])
        start += gradient.shape[1]
        if results:
            gradient, results[-1] = lax.optimization_barrier((gradient, results[-1]))
        updated = adamw(
            gradient * scaling,
            params[:, cut],
            first_moment[:, cut],
            second_moment[:, cut],
            key_params[:, cut],
        )
        codes = ring_codes(updated[3].astype(jnp.bfloat16), encoded_rows)
        normed = batch_norm(codes.astype(jnp.bfloat16), bn_gain[cut], bn_shift[cut])
        results.append(updated + (normed,))
    new_params, new_first, new_second, new_key, normed = (
        jnp.concatenate(parts, axis=1) for parts in zip(*results)
    )
    returned = lax.all_to_all(
        jnp.take(normed, send_back, axis=0), DP, split_axis=0, concat_axis=0, tiled=True
    )
    restored = jnp.take(returned, receive_back, axis=0)
    new_queue = lax.dynamic_update_slice(
        queue, restored[None], (slot[0], jnp.int32(0), jnp.int32(0))
    )
    return (new_params, new_first, new_second, new_key, new_queue)


def solution(mesh):
    groups, dp = mesh.devices.shape
    grid = Mesh(mesh.devices.reshape(groups, dp // 4, 2, 2), ("groups",) + DP)
    rows = P(("groups",) + DP, None)
    in_specs = (
        rows,
        rows,
        rows,
        rows,
        rows,
        rows,
        rows,
        P("groups"),
        P("groups"),
        P("groups"),
        P("groups"),
        P("groups", DP, None),
        P(),
    )
    out_specs = (rows, rows, rows, rows, P("groups", DP, None))
    return jax.shard_map(
        per_device, mesh=grid, in_specs=in_specs, out_specs=out_specs, check_vma=False
    )
```

```python
import jax
import jax.numpy as jnp
from jax import lax
from jax.sharding import Mesh
from jax.sharding import PartitionSpec as P

norm_epsilon = 1e-05
adam_epsilon = 1e-08
bias_first = 1.0 - 0.9**10
bias_second = 1.0 - 0.999**10

DP = ("zo", "xl", "c")


def route(mapping, position, block_rows, per_peer):
    members = mapping.shape[0] // block_rows
    layout = mapping.reshape(members, block_rows)
    owned = layout // block_rows == position
    ordinal = jnp.cumsum(owned.astype(jnp.int32), axis=1) - 1
    offsets = layout - position * block_rows
    slots = jnp.arange(per_peer, dtype=jnp.int32)[None, :, None]
    hit = owned[:, None, :] & (ordinal[:, None, :] == slots)
    send_index = jnp.sum(jnp.where(hit, offsets[:, None, :], 0), axis=2).reshape(-1)
    own_block = lax.dynamic_slice_in_dim(mapping, position * block_rows, block_rows)
    anchor = own_block // block_rows
    indicator = (anchor[:, None] == jnp.arange(members, dtype=jnp.int32)[None, :]).astype(jnp.int32)
    arrival = jnp.sum((jnp.cumsum(indicator, axis=0) - 1) * indicator, axis=1)
    return (send_index, anchor * per_peer + arrival)


def pair_gradient(queries, grad_out):
    tokens, width = queries.shape
    zo = lax.axis_size("zo")
    x = lax.axis_index("xl")
    blocks = queries.reshape(tokens, zo, 2, 2, width // (4 * zo))
    mine = lax.dynamic_index_in_dim(blocks, x, axis=2, keepdims=False)
    theirs = lax.dynamic_index_in_dim(blocks, 1 - x, axis=2, keepdims=False)
    mine = mine.reshape(tokens, width // 2)
    theirs = theirs.reshape(tokens, width // 2)
    swap = [(0, 1), (1, 0)]
    half = grad_out.shape[1] * 3 // 8
    got_queries, got_first = lax.ppermute((theirs, grad_out[:, :half]), "xl", swap)
    got_second = lax.ppermute(grad_out[:, half:], "xl", swap)
    both_queries = jnp.concatenate([mine, got_queries], axis=0)
    parts = []
    for own, got in ((grad_out[:, :half], got_first), (grad_out[:, half:], got_second)):
        partial = lax.dot_general(
            both_queries,
            jnp.concatenate([own, got], axis=0),
            (((0,), (0,)), ((), ())),
            preferred_element_type=jnp.float32,
        )
        parts.append(lax.psum_scatter(partial, ("zo", "c"), scatter_dimension=0, tiled=True))
    return parts


def ring_codes(weight, rows):
    zo_size = lax.axis_size("zo")
    length = 2 * zo_size
    block = weight.shape[0]

    def where(q):
        return (q if q < zo_size else length - 1 - q, 0 if q < zo_size else 1)

    def index(zo, xl, c):
        return (zo * 2 + xl) * 2 + c

    def pairs(step):
        return [
            (index(*where(q), c), index(*where((q + step) % length), c))
            for q in range(length)
            for c in (0, 1)
        ]

    forward, backward = pairs(1), pairs(length - 1)
    partner = [
        (index(zo, xl, c), index(zo, xl, 1 - c))
        for zo in range(zo_size)
        for xl in (0, 1)
        for c in (0, 1)
    ]
    zo = lax.axis_index("zo")
    xl = lax.axis_index("xl")
    c = lax.axis_index("c")
    here = jnp.where(xl == 0, zo, length - 1 - zo)

    def columns(offset, cls):
        q = (here + offset) % length
        source = jnp.where(q < zo_size, q, length - 1 - q)
        source = (source * 2 + (q >= zo_size).astype(jnp.int32)) * 2 + cls
        return lax.dynamic_slice_in_dim(rows, source * block, block, axis=1)

    def add(total, offset, cls, shard):
        part = jnp.dot(columns(offset, cls), shard, preferred_element_type=jnp.float32)
        return part if total is None else total + part

    total = add(None, 0, c, weight)
    ahead, behind = weight, weight
    handed = [(0, weight)]
    for step in range(1, length // 2 + 1):
        sent = lax.ppermute(tuple(s for _, s in handed), DP, partner)
        for (offset, _), shard in zip(handed, sent):
            total = add(total, offset, 1 - c, shard)
        handed = []
        ahead = lax.ppermute(ahead, DP, forward)
        total = add(total, -step, c, ahead)
        handed.append((-step, ahead))
        if step < length // 2:
            behind = lax.ppermute(behind, DP, backward)
            total = add(total, step, c, behind)
            handed.append((step, behind))
    sent = lax.ppermute(tuple(s for _, s in handed), DP, partner)
    for (offset, _), shard in zip(handed, sent):
        total = add(total, offset, 1 - c, shard)
    return total


def adamw(gradient, params, first_moment, second_moment, key_params):
    new_first = 0.9 * first_moment + 0.1 * gradient
    new_second = 0.999 * second_moment + 0.001 * gradient * gradient
    update = new_first / bias_first / (jnp.sqrt(new_second / bias_second) + adam_epsilon)
    new_params = params - 0.05 * (update + 0.1 * params)
    new_key = 0.99 * key_params + 0.01 * new_params
    return (new_params, new_first, new_second, new_key)


def batch_norm(codes, bn_gain, bn_shift):
    values = codes.astype(jnp.float32)
    center = jnp.mean(values, axis=0)
    spread = jnp.mean(jnp.square(values - center), axis=0)
    return jax.nn.relu(
        (values - center) * lax.rsqrt(spread + norm_epsilon) * bn_gain + bn_shift
    ).astype(jnp.bfloat16)


def per_device(
    queries,
    grad_out,
    params,
    first_moment,
    second_moment,
    key_params,
    keys,
    perm,
    inv_perm,
    bn_gain,
    bn_shift,
    queue,
    slot,
):
    position = lax.axis_index(DP)
    members = lax.axis_size(DP)
    block_rows = keys.shape[0]
    per_peer = block_rows // members
    scaling = 1.0 / jnp.sqrt(jnp.float32(queries.shape[0] * members))
    send_forward, receive_forward = route(perm, position, block_rows, per_peer)
    send_back, receive_back = route(inv_perm, position, block_rows, per_peer)
    moved = lax.all_to_all(
        jnp.take(keys, send_forward, axis=0), DP, split_axis=0, concat_axis=0, tiled=True
    )
    encoded_rows = jnp.take(moved, receive_forward, axis=0)
    halves = pair_gradient(queries, grad_out)
    halves[0], (encoded_rows, send_back, receive_back) = lax.optimization_barrier(
        (halves[0], (encoded_rows, send_back, receive_back))
    )
    kept = encoded_rows[0, 0] == encoded_rows[0, 0]
    queue = lax.optimization_barrier(jnp.where(kept, queue, jnp.zeros_like(queue)))
    results = []
    start = 0
    for gradient in halves:
        cut = slice(start, start + gradient.shape[1])
        start += gradient.shape[1]
        if results:
            gradient, results[-1] = lax.optimization_barrier((gradient, results[-1]))
        updated = adamw(
            gradient * scaling,
            params[:, cut],
            first_moment[:, cut],
            second_moment[:, cut],
            key_params[:, cut],
        )
        codes = ring_codes(updated[3].astype(jnp.bfloat16), encoded_rows)
        normed = batch_norm(codes.astype(jnp.bfloat16), bn_gain[cut], bn_shift[cut])
        results.append(updated + (normed,))
    new_params, new_first, new_second, new_key, normed = (
        jnp.concatenate(parts, axis=1) for parts in zip(*results)
    )
    returned = lax.all_to_all(
        jnp.take(normed, send_back, axis=0), DP, split_axis=0, concat_axis=0, tiled=True
    )
    restored = jnp.take(returned, receive_back, axis=0)
    new_queue = lax.dynamic_update_slice(
        queue, restored[None], (slot[0], jnp.int32(0), jnp.int32(0))
    )
    return (new_params, new_first, new_second, new_key, new_queue)


def solution(mesh):
    groups, dp = mesh.devices.shape
    grid = Mesh(mesh.devices.reshape(groups, dp // 4, 2, 2), ("groups",) + DP)
    rows = P(("groups",) + DP, None)
    in_specs = (
        rows,
        rows,
        rows,
        rows,
        rows,
        rows,
        rows,
        P("groups"),
        P("groups"),
        P("groups"),
        P("groups"),
        P("groups", DP, None),
        P(),
    )
    out_specs = (rows, rows, rows, rows, P("groups", DP, None))
    return jax.shard_map(
        per_device, mesh=grid, in_specs=in_specs, out_specs=out_specs, check_vma=False
    )
```
